32 devices in a mesh: groups: 2 (over y), rows: 8 (over z, x), heads: 2 (over core).
Axes of the slice: x: 2, y: 2, z: 4, core: 2. Of those that a mesh axis runs over, the one named last changes fastest.
Arguments:
- residual_in: bfloat16 [128, 8192], P(('groups', 'rows'), 'heads'), parts along dimension 0, may hold values from -6 to 6
- query: bfloat16 [128, 8192], P(('groups', 'rows'), 'heads'), parts along dimension 0, may hold values from -120 to 120
- key_cache: bfloat16 [128, 4, 32, 128], P(('groups', 'rows'), 'heads'), parts along dimension 0, may hold values from -4 to 4
- value_cache: bfloat16 [128, 4, 32, 128], P(('groups', 'rows'), 'heads'), parts along dimension 0, may hold values from -5 to 5
- key_new: bfloat16 [128, 4, 128], P(('groups', 'rows'), 'heads'), parts along dimension 0, may hold values from -4 to 4
- value_new: bfloat16 [128, 4, 128], P(('groups', 'rows'), 'heads'), parts along dimension 0, may hold values from -5 to 5
- lengths: int32 [128], P(('groups', 'rows')), parts along dimension 0, may hold values from 2 to 32, as said below
- norm_gain: bfloat16 [8192], replicated, may hold values from 0.3984375 to 1.59375
- hot_gate: bfloat16 [128, 8192], P('heads'), may hold values from -0.0625 to 0.0625
- hot_up: bfloat16 [128, 8192], P('heads'), may hold values from -0.0625 to 0.0625
- hot_down: bfloat16 [128, 8192], P('heads'), may hold values from -0.5 to 0.5
- cold_gate: bfloat16 [512, 8192], P(('rows', 'heads')), may hold values from -0.0625 to 0.0625
- cold_up: bfloat16 [512, 8192], P(('rows', 'heads')), may hold values from -0.0625 to 0.0625
- cold_down: bfloat16 [512, 8192], P(('rows', 'heads')), may hold values from -0.5 to 0.5
- active: int32 [128, 4], P(('groups', 'rows')), parts along dimension 0, may hold values from 0 to 1, as said below
Outputs:
- residual_out: bfloat16 [128, 8192], P(('groups', 'rows'), 'heads'), parts along dimension 0
The draws below stay inside these ranges and needn't reach their ends.
There are 2 independent parts, one for each index of `groups`. The reference program is written for one: setup_inputs(seed, part) draws one part's arguments, and reference() takes and returns one part's arrays. A program takes and returns all parts, laid end to end along the dimension named above; an argument that names none is the same for every part. Nothing has to cross between parts.
Inputs may be any that keep to these rules, and one draw needn't show every extreme that they name: `lengths`: every request has at least two filled slots, and some request has all 32. `active`: 0 or 1; among the 8 requests of one index of rows at most 2 are active on any one cold block, and exactly 2 on some.
All inputs are finite; a program needn't handle non-finite values.
Results may differ from the reference program's by a relative error of at most 0.0085.
Values may be sent and summed in bfloat16 or wider, within the bound.
No kernel may reach another device: no remote copies, remote signals or barrier semaphores. Data moves between devices by JAX's collectives and lax.ppermute only.
A program may use at most 64 MiB of HBM per device.

```python
import jax
import jax.numpy as jnp
from jax import lax

HD = 128
QH = 64
KVH = 4
D = 8192
GROUP = 16
BLOCK = 128
HOT = 1
CAP = 2
REQ_DEV = 8
CTX = 32
REQS = 64
NCOLD = 4


def shared_pair(key):
    keys_all = jnp.clip(jax.random.normal(jax.random.fold_in(key, 11), (REQS, KVH, CTX, HD), jnp.float32), -4.0, 4.0)
    queries = jnp.clip(jax.random.normal(jax.random.fold_in(key, 12), (REQS, QH, HD), jnp.float32), -4.0, 4.0)
    return (queries.reshape(REQS, QH * HD), keys_all)


def draw_query(key, part):
    return shared_pair(key)[0].astype(jnp.bfloat16)


def draw_key_cache(key, part):
    return shared_pair(key)[1].astype(jnp.bfloat16)


def draw_lengths(key, part):
    drawn = jax.random.randint(jax.random.fold_in(key, 21), (REQS,), 2, CTX + 1)
    return drawn.at[0].set(CTX).astype(jnp.int32)


def draw_active(key, part):
    owners = REQS // REQ_DEV
    levels = jax.random.randint(jax.random.fold_in(key, 32), (NCOLD,), 1, 7)
    rolled = jax.random.randint(jax.random.fold_in(key, 31), (REQS, NCOLD), 0, 16)
    switched = (rolled < levels[None, :]).astype(jnp.int32)
    switched = switched.at[0:CAP, 0].set(1)
    grouped = switched.reshape(owners, REQ_DEV, NCOLD)
    before = jnp.cumsum(grouped, axis=1) - grouped
    kept = grouped * (before < CAP).astype(jnp.int32)
    return kept.reshape(REQS, NCOLD).astype(jnp.int32)


def block_scale(key, dims, split, low, top_value):
    factor_of, own = 1.0, jax.random.fold_in(key, 6)
    for position, blocks in split:
        draws = jnp.exp(jax.random.uniform(jax.random.fold_in(own, position), (blocks,), jnp.float32, low / len(split), top_value / len(split)))
        factor_of = factor_of * jnp.repeat(draws, dims[position] // blocks).reshape([-1 if axis == position else 1 for axis in range(len(dims))])
    return factor_of


def bell_draw(own_key, extent, scale, most, split=(), held_as=jnp.bfloat16):
    factor_of = block_scale(own_key, extent, split, -0.22, 0.18) if split else 1.0
    array = jax.random.normal(own_key, extent, jnp.float32) * scale * factor_of
    return jnp.minimum(jnp.maximum(array, -most), most).astype(held_as)


def setup_inputs(seed: int = 0, part: int = 0) -> dict:
    keys = jax.random.split(jax.random.key(seed), 16)
    part_keys = jax.random.split(jax.random.fold_in(keys[15], part), 16)
    residual_in = bell_draw(part_keys[0], (REQS, D), 1.0, 6.0, ((0, 8), (1, 2)))
    query = draw_query(jax.random.fold_in(jax.random.fold_in(keys[15], part), 71), part)
    key_cache = draw_key_cache(jax.random.fold_in(jax.random.fold_in(keys[15], part), 71), part)
    value_cache = bell_draw(part_keys[3], (REQS, KVH, CTX, HD), 1.0, 5.0, ((0, 8), (1, 2)))
    key_new = bell_draw(part_keys[4], (REQS, KVH, HD), 1.0, 4.0, ((0, 8), (1, 2)))
    value_new = bell_draw(part_keys[5], (REQS, KVH, HD), 1.0, 5.0, ((0, 8), (1, 2)))
    lengths = draw_lengths(jax.random.fold_in(jax.random.fold_in(keys[15], part), 71), part)
    norm_gain = jnp.clip(1.0 + 0.12 * jax.random.normal(keys[7], (D,), jnp.float32), 0.3984375, 1.59375).astype(jnp.bfloat16)
    hot_gate = bell_draw(keys[8], (HOT * BLOCK, D), D ** -0.5, 0.0625, ((0, 2),))
    hot_up = bell_draw(keys[9], (HOT * BLOCK, D), D ** -0.5, 0.0625, ((0, 2),))
    hot_down = bell_draw(keys[10], (HOT * BLOCK, D), BLOCK ** -0.5, 0.5, ((0, 2),))
    cold_gate = bell_draw(keys[11], (NCOLD * BLOCK, D), D ** -0.5, 0.0625, ((0, 16),))
    cold_up = bell_draw(keys[12], (NCOLD * BLOCK, D), D ** -0.5, 0.0625, ((0, 16),))
    cold_down = bell_draw(keys[13], (NCOLD * BLOCK, D), BLOCK ** -0.5, 0.5, ((0, 16),))
    active = draw_active(jax.random.fold_in(jax.random.fold_in(keys[15], part), 71), part)
    return {"residual_in": residual_in, "query": query, "key_cache": key_cache, "value_cache": value_cache, "key_new": key_new, "value_new": value_new, "lengths": lengths, "norm_gain": norm_gain, "hot_gate": hot_gate, "hot_up": hot_up, "hot_down": hot_down, "cold_gate": cold_gate, "cold_up": cold_up, "cold_down": cold_down, "active": active}


def attention_rows(query, key_cache, value_cache, key_new, value_new, lengths):
    count = query.shape[0]
    scale_factor = 1.0 / HD ** 0.5
    queries = query.astype(jnp.float32).reshape(count, KVH, GROUP, HD)
    scores = jnp.einsum('rgjd,rgpd->rgjp', queries, key_cache.astype(jnp.float32)) * scale_factor
    own_score = jnp.einsum('rgjd,rgd->rgj', queries, key_new.astype(jnp.float32)) * scale_factor
    visible = (jnp.arange(CTX, dtype=jnp.int32)[None, :] < lengths[:, None])[:, None, None, :]
    scores = jnp.where(visible, scores, -1e+30)
    highest = jnp.maximum(lax.optimization_barrier(jnp.max(scores, axis=-1)), own_score)
    expons = jnp.where(visible, jnp.exp(scores - highest[..., None]), 0.0)
    own_expon = jnp.exp(own_score - highest)
    totals = lax.optimization_barrier(jnp.sum(expons, axis=-1)) + own_expon
    weights = (expons / totals[..., None]).astype(jnp.bfloat16)
    own_weight = (own_expon / totals).astype(jnp.bfloat16)
    blended = jnp.einsum('rgjp,rgpd->rgjd', weights.astype(jnp.float32), value_cache.astype(jnp.float32))
    blended = blended + own_weight.astype(jnp.float32)[..., None] * value_new.astype(jnp.float32)[:, :, None, :]
    return blended.reshape(count, QH * HD)

def swiglu(normed, gate_rows, up_rows):
    gate = jnp.dot(normed, gate_rows.T, preferred_element_type=jnp.float32)
    upper = jnp.dot(normed, up_rows.T, preferred_element_type=jnp.float32)
    return jax.nn.silu(gate) * upper

def reference(residual_in, query, key_cache, value_cache, key_new, value_new, lengths, norm_gain, hot_gate, hot_up, hot_down, cold_gate, cold_up, cold_down, active):
    attended = attention_rows(query, key_cache, value_cache, key_new, value_new, lengths)
    stream = (residual_in.astype(jnp.float32) + attended).astype(jnp.bfloat16)
    wide = stream.astype(jnp.float32)
    mean_sq = lax.optimization_barrier(jnp.mean(wide * wide, axis=-1, keepdims=True))
    normed = (wide * jax.lax.rsqrt(mean_sq + 1e-05) * norm_gain.astype(jnp.float32)).astype(jnp.bfloat16)
    hot_hidden = swiglu(normed, hot_gate, hot_up).astype(jnp.bfloat16)
    hot_part = jnp.dot(hot_hidden, hot_down, preferred_element_type=jnp.float32)
    neuron_mask = jnp.repeat(active.astype(jnp.float32), BLOCK, axis=1)
    cold_hidden = (swiglu(normed, cold_gate, cold_up) * neuron_mask).astype(jnp.bfloat16)
    cold_part = jnp.dot(cold_hidden, cold_down, preferred_element_type=jnp.float32)
    return (stream.astype(jnp.float32) + hot_part + cold_part).astype(jnp.bfloat16)
```

```python
import jax
import jax.numpy as jnp
from jax import lax
from jax.sharding import PartitionSpec as P

HD = 128
D = 8192
CAP = 2


def partner(block, axis, bit):
    count = lax.axis_size(axis)
    route = []
    for low in range(count):
        high = low | 1 << bit
        if high != low and high < count:
            route += [(low, high), (high, low)]
    return lax.ppermute(block, axis, route)


def join_halves(half, myself):
    other = partner(half, "heads", 0)
    low_first = jnp.concatenate([half, other], axis=1)
    high_first = jnp.concatenate([other, half], axis=1)
    return jnp.where(myself == 0, low_first, high_first)


def attention_rows(query, key_cache, value_cache, key_new, value_new, lengths):
    count = key_cache.shape[0]
    kv_local = key_cache.shape[1]
    scale_factor = 1.0 / HD**0.5
    queries = query.reshape(count, kv_local, -1, HD)
    scores = (
        jnp.einsum("rgjd,rgpd->rgjp", queries, key_cache, preferred_element_type=jnp.float32)
        * scale_factor
    )
    own_score = (
        jnp.einsum("rgjd,rgd->rgj", queries, key_new, preferred_element_type=jnp.float32)
        * scale_factor
    )
    visible = (jnp.arange(key_cache.shape[2], dtype=jnp.int32)[None, :] < lengths[:, None])[
        :, None, None, :
    ]
    scores = jnp.where(visible, scores, -1e30)
    highest = jnp.maximum(jnp.max(scores, axis=-1), own_score)
    expons = jnp.where(visible, jnp.exp(scores - highest[..., None]), 0.0)
    own_expon = jnp.exp(own_score - highest)
    totals = jnp.sum(expons, axis=-1) + own_expon
    weights = (expons / totals[..., None]).astype(jnp.bfloat16)
    own_weight = (own_expon / totals).astype(jnp.bfloat16)
    blended = jnp.einsum(
        "rgjp,rgpd->rgjd", weights, value_cache, preferred_element_type=jnp.float32
    )
    blended = (
        blended
        + own_weight.astype(jnp.float32)[..., None] * value_new.astype(jnp.float32)[:, :, None, :]
    )
    return blended.reshape(count, -1)


def swiglu_rows(normed, gate_rows, up_rows, down_rows):
    gate = jnp.einsum("rd,nd->rn", normed, gate_rows, preferred_element_type=jnp.float32)
    upper = jnp.einsum("rd,nd->rn", normed, up_rows, preferred_element_type=jnp.float32)
    hidden = (jax.nn.silu(gate) * upper).astype(jnp.bfloat16)
    return jnp.dot(hidden, down_rows, preferred_element_type=jnp.float32)


def collect_rows(selector, returned):
    return lax.dot_general(
        selector,
        returned,
        (((0,), (0,)), ((), ())),
        precision=lax.Precision.HIGHEST,
        preferred_element_type=jnp.float32,
    )


def local(
    residual_in,
    query,
    key_cache,
    value_cache,
    key_new,
    value_new,
    lengths,
    norm_gain,
    hot_gate,
    hot_up,
    hot_down,
    cold_gate,
    cold_up,
    cold_down,
    active,
):
    attended = attention_rows(query, key_cache, value_cache, key_new, value_new, lengths)
    stream = (residual_in.astype(jnp.float32) + attended).astype(jnp.bfloat16)
    half_width = stream.shape[1]
    myself = lax.axis_index("heads")
    local_wide = stream.astype(jnp.float32)
    square_part = jnp.sum(local_wide * local_wide, axis=-1)
    square_total = square_part + partner(square_part, "heads", 0)
    gain_half = lax.dynamic_slice_in_dim(norm_gain, myself * half_width, half_width)
    scaled = (
        local_wide * lax.rsqrt(square_total / D + 1e-05)[:, None] * gain_half.astype(jnp.float32)
    )
    normed = join_halves(scaled.astype(jnp.bfloat16), myself)
    hot_part = swiglu_rows(normed, hot_gate, hot_up, hot_down)
    owner_count = lax.axis_size("rows")
    block_count = active.shape[1]
    request_count = active.shape[0]
    by_block = jnp.transpose(active)
    earlier = jnp.cumsum(by_block, axis=1) - by_block
    slot_ids = jnp.arange(CAP, dtype=jnp.int32)[None, :, None]
    slot_table = by_block[:, None, :] * (earlier[:, None, :] == slot_ids).astype(jnp.int32)
    selector = jnp.repeat(slot_table, owner_count // block_count, axis=0).reshape(
        owner_count * CAP, request_count
    )
    outgoing = jnp.dot(
        selector.astype(jnp.bfloat16), normed, preferred_element_type=jnp.float32
    ).astype(jnp.bfloat16)
    incoming = lax.all_to_all(outgoing, "rows", split_axis=0, concat_axis=0, tiled=True)
    cold_part = swiglu_rows(incoming, cold_gate, cold_up, cold_down)
    selector_wide = selector.astype(jnp.float32)
    kept = lax.dynamic_slice_in_dim(cold_part, myself * half_width, half_width, 1)
    given = lax.dynamic_slice_in_dim(cold_part, (1 - myself) * half_width, half_width, 1)
    owner_sum = kept + partner(given, "heads", 0)
    returned = lax.all_to_all(owner_sum, "rows", split_axis=0, concat_axis=0, tiled=True)
    cold_sum = collect_rows(selector_wide, returned)
    hot_kept = lax.dynamic_slice_in_dim(hot_part, myself * half_width, half_width, 1)
    hot_given = lax.dynamic_slice_in_dim(hot_part, (1 - myself) * half_width, half_width, 1)
    hot_total = hot_kept + partner(hot_given, "heads", 0)
    result = stream.astype(jnp.float32) + hot_total + cold_sum
    return result.astype(jnp.bfloat16)


def solution(mesh):
    return jax.shard_map(
        local,
        mesh=mesh,
        in_specs=(
            P(("groups", "rows"), "heads"),
            P(("groups", "rows"), "heads"),
            P(("groups", "rows"), "heads", None, None),
            P(("groups", "rows"), "heads", None, None),
            P(("groups", "rows"), "heads", None),
            P(("groups", "rows"), "heads", None),
            P(("groups", "rows")),
            P(),
            P("heads", None),
            P("heads", None),
            P("heads", None),
            P(("rows", "heads"), None),
            P(("rows", "heads"), None),
            P(("rows", "heads"), None),
            P(("groups", "rows"), None),
        ),
        out_specs=P(("groups", "rows"), "heads"),
        check_vma=False,
    )
```

```python
import jax
import jax.numpy as jnp
from jax import lax
from jax.sharding import PartitionSpec as P

HD = 128
D = 8192
CAP = 2


def partner(block, axis, bit):
    count = lax.axis_size(axis)
    route = []
    for low in range(count):
        high = low | 1 << bit
        if high != low and high < count:
            route += [(low, high), (high, low)]
    return lax.ppermute(block, axis, route)


def join_halves(half, myself):
    other = partner(half, "heads", 0)
    low_first = jnp.concatenate([half, other], axis=1)
    high_first = jnp.concatenate([other, half], axis=1)
    return jnp.where(myself == 0, low_first, high_first)


def attention_rows(query, key_cache, value_cache, key_new, value_new, lengths):
    count = key_cache.shape[0]
    kv_local = key_cache.shape[1]
    scale_factor = 1.0 / HD**0.5
    queries = query.reshape(count, kv_local, -1, HD)
    scores = (
        jnp.einsum("rgjd,rgpd->rgjp", queries, key_cache, preferred_element_type=jnp.float32)
        * scale_factor
    )
    own_score = (
        jnp.einsum("rgjd,rgd->rgj", queries, key_new, preferred_element_type=jnp.float32)
        * scale_factor
    )
    visible = (jnp.arange(key_cache.shape[2], dtype=jnp.int32)[None, :] < lengths[:, None])[
        :, None, None, :
    ]
    scores = jnp.where(visible, scores, -1e30)
    highest = jnp.maximum(jnp.max(scores, axis=-1), own_score)
    expons = jnp.where(visible, jnp.exp(scores - highest[..., None]), 0.0)
    own_expon = jnp.exp(own_score - highest)
    totals = jnp.sum(expons, axis=-1) + own_expon
    weights = (expons / totals[..., None]).astype(jnp.bfloat16)
    own_weight = (own_expon / totals).astype(jnp.bfloat16)
    blended = jnp.einsum(
        "rgjp,rgpd->rgjd", weights, value_cache, preferred_element_type=jnp.float32
    )
    blended = (
        blended
        + own_weight.astype(jnp.float32)[..., None] * value_new.astype(jnp.float32)[:, :, None, :]
    )
    return blended.reshape(count, -1)


def swiglu_rows(normed, gate_rows, up_rows, down_rows):
    gate = jnp.einsum("rd,nd->rn", normed, gate_rows, preferred_element_type=jnp.float32)
    upper = jnp.einsum("rd,nd->rn", normed, up_rows, preferred_element_type=jnp.float32)
    hidden = (jax.nn.silu(gate) * upper).astype(jnp.bfloat16)
    return jnp.dot(hidden, down_rows, preferred_element_type=jnp.float32)


def collect_rows(selector, returned):
    return lax.dot_general(
        selector,
        returned,
        (((0,), (0,)), ((), ())),
        precision=lax.Precision.HIGHEST,
        preferred_element_type=jnp.float32,
    )


def local(
    residual_in,
    query,
    key_cache,
    value_cache,
    key_new,
    value_new,
    lengths,
    norm_gain,
    hot_gate,
    hot_up,
    hot_down,
    cold_gate,
    cold_up,
    cold_down,
    active,
):
    attended = attention_rows(query, key_cache, value_cache, key_new, value_new, lengths)
    stream = (residual_in.astype(jnp.float32) + attended).astype(jnp.bfloat16)
    half_width = stream.shape[1]
    myself = lax.axis_index("heads")
    local_wide = stream.astype(jnp.float32)
    square_part = jnp.sum(local_wide * local_wide, axis=-1)
    square_total = square_part + partner(square_part, "heads", 0)
    gain_half = lax.dynamic_slice_in_dim(norm_gain, myself * half_width, half_width)
    scaled = (
        local_wide * lax.rsqrt(square_total / D + 1e-05)[:, None] * gain_half.astype(jnp.float32)
    )
    normed = join_halves(scaled.astype(jnp.bfloat16), myself)
    hot_part = swiglu_rows(normed, hot_gate, hot_up, hot_down)
    owner_count = lax.axis_size("rows")
    block_count = active.shape[1]
    request_count = active.shape[0]
    by_block = jnp.transpose(active)
    earlier = jnp.cumsum(by_block, axis=1) - by_block
    slot_ids = jnp.arange(CAP, dtype=jnp.int32)[None, :, None]
    slot_table = by_block[:, None, :] * (earlier[:, None, :] == slot_ids).astype(jnp.int32)
    selector = jnp.repeat(slot_table, owner_count // block_count, axis=0).reshape(
        owner_count * CAP, request_count
    )
    outgoing = jnp.dot(
        selector.astype(jnp.bfloat16), scaled.astype(jnp.bfloat16), preferred_element_type=jnp.float32
    ).astype(jnp.bfloat16)
    incoming_half = lax.all_to_all(outgoing, "rows", split_axis=0, concat_axis=0, tiled=True)
    incoming = join_halves(incoming_half, myself)
    cold_part = swiglu_rows(incoming, cold_gate, cold_up, cold_down)
    selector_wide = selector.astype(jnp.float32)
    kept = lax.dynamic_slice_in_dim(cold_part, myself * half_width, half_width, 1)
    given = lax.dynamic_slice_in_dim(cold_part, (1 - myself) * half_width, half_width, 1)
    owner_sum = kept + partner(given, "heads", 0)
    returned = lax.all_to_all(
        owner_sum.astype(jnp.bfloat16), "rows", split_axis=0, concat_axis=0, tiled=True
    )
    cold_sum = collect_rows(selector_wide, returned.astype(jnp.float32))
    hot_kept = lax.dynamic_slice_in_dim(hot_part, myself * half_width, half_width, 1)
    hot_given = lax.dynamic_slice_in_dim(hot_part, (1 - myself) * half_width, half_width, 1)
    hot_total = hot_kept + partner(hot_given, "heads", 0)
    result = stream.astype(jnp.float32) + hot_total + cold_sum
    return result.astype(jnp.bfloat16)


def solution(mesh):
    return jax.shard_map(
        local,
        mesh=mesh,
        in_specs=(
            P(("groups", "rows"), "heads"),
            P(("groups", "rows"), "heads"),
            P(("groups", "rows"), "heads", None, None),
            P(("groups", "rows"), "heads", None, None),
            P(("groups", "rows"), "heads", None),
            P(("groups", "rows"), "heads", None),
            P(("groups", "rows")),
            P(),
            P("heads", None),
            P("heads", None),
            P("heads", None),
            P(("rows", "heads"), None),
            P(("rows", "heads"), None),
            P(("rows", "heads"), None),
            P(("groups", "rows"), None),
        ),
        out_specs=P(("groups", "rows"), "heads"),
        check_vma=False,
    )
```

```python
import jax
import jax.numpy as jnp
from jax import lax
from jax.sharding import PartitionSpec as P

HD = 128
D = 8192
CAP = 2


def partner(block, axis, bit):
    count = lax.axis_size(axis)
    route = []
    for low in range(count):
        high = low | 1 << bit
        if high != low and high < count:
            route += [(low, high), (high, low)]
    return lax.ppermute(block, axis, route)


def join_halves(half, myself):
    other = partner(half, "heads", 0)
    low_first = jnp.concatenate([half, other], axis=1)
    high_first = jnp.concatenate([other, half], axis=1)
    return jnp.where(myself == 0, low_first, high_first)


def attention_rows(query, key_cache, value_cache, key_new, value_new, lengths):
    count = key_cache.shape[0]
    kv_local = key_cache.shape[1]
    scale_factor = 1.0 / HD**0.5
    queries = query.reshape(count, kv_local, -1, HD)
    scores = (
        jnp.einsum("rgjd,rgpd->rgjp", queries, key_cache, preferred_element_type=jnp.float32)
        * scale_factor
    )
    own_score = (
        jnp.einsum("rgjd,rgd->rgj", queries, key_new, preferred_element_type=jnp.float32)
        * scale_factor
    )
    visible = (jnp.arange(key_cache.shape[2], dtype=jnp.int32)[None, :] < lengths[:, None])[
        :, None, None, :
    ]
    scores = jnp.where(visible, scores, -1e30)
    highest = jnp.maximum(jnp.max(scores, axis=-1), own_score)
    expons = jnp.where(visible, jnp.exp(scores - highest[..., None]), 0.0)
    own_expon = jnp.exp(own_score - highest)
    totals = jnp.sum(expons, axis=-1) + own_expon
    weights = (expons / totals[..., None]).astype(jnp.bfloat16)
    own_weight = (own_expon / totals).astype(jnp.bfloat16)
    blended = jnp.einsum(
        "rgjp,rgpd->rgjd", weights, value_cache, preferred_element_type=jnp.float32
    )
    blended = (
        blended
        + own_weight.astype(jnp.float32)[..., None] * value_new.astype(jnp.float32)[:, :, None, :]
    )
    return blended.reshape(count, -1)


def swiglu_rows(normed, gate_rows, up_rows, down_rows):
    gate = jnp.einsum("rd,nd->rn", normed, gate_rows, preferred_element_type=jnp.float32)
    upper = jnp.einsum("rd,nd->rn", normed, up_rows, preferred_element_type=jnp.float32)
    hidden = (jax.nn.silu(gate) * upper).astype(jnp.bfloat16)
    return jnp.dot(hidden, down_rows, preferred_element_type=jnp.float32)


def swiglu_halves(normed, gate_rows, up_rows, down_rows, myself):
    gate = jnp.einsum("rd,nd->rn", normed, gate_rows, preferred_element_type=jnp.float32)
    upper = jnp.einsum("rd,nd->rn", normed, up_rows, preferred_element_type=jnp.float32)
    hidden = (jax.nn.silu(gate) * upper).astype(jnp.bfloat16)
    half_width = down_rows.shape[1] // 2
    down_given = lax.dynamic_slice_in_dim(down_rows, (1 - myself) * half_width, half_width, 1)
    down_kept = lax.dynamic_slice_in_dim(down_rows, myself * half_width, half_width, 1)
    given = jnp.dot(hidden, down_given, preferred_element_type=jnp.float32)
    kept = jnp.dot(hidden, down_kept, preferred_element_type=jnp.float32)
    return kept, given


def collect_rows(selector, returned):
    return lax.dot_general(
        selector,
        returned,
        (((0,), (0,)), ((), ())),
        precision=lax.Precision.HIGHEST,
        preferred_element_type=jnp.float32,
    )


def local(
    residual_in,
    query,
    key_cache,
    value_cache,
    key_new,
    value_new,
    lengths,
    norm_gain,
    hot_gate,
    hot_up,
    hot_down,
    cold_gate,
    cold_up,
    cold_down,
    active,
):
    attended = attention_rows(query, key_cache, value_cache, key_new, value_new, lengths)
    stream = (residual_in.astype(jnp.float32) + attended).astype(jnp.bfloat16)
    half_width = stream.shape[1]
    myself = lax.axis_index("heads")
    local_wide = stream.astype(jnp.float32)
    square_part = jnp.sum(local_wide * local_wide, axis=-1)
    square_total = square_part + partner(square_part, "heads", 0)
    gain_half = lax.dynamic_slice_in_dim(norm_gain, myself * half_width, half_width)
    scaled = (
        local_wide * lax.rsqrt(square_total / D + 1e-05)[:, None] * gain_half.astype(jnp.float32)
    )
    normed = join_halves(scaled.astype(jnp.bfloat16), myself)
    owner_count = lax.axis_size("rows")
    block_count = active.shape[1]
    request_count = active.shape[0]
    by_block = jnp.transpose(active)
    earlier = jnp.cumsum(by_block, axis=1) - by_block
    slot_ids = jnp.arange(CAP, dtype=jnp.int32)[None, :, None]
    slot_table = by_block[:, None, :] * (earlier[:, None, :] == slot_ids).astype(jnp.int32)
    selector3 = jnp.repeat(slot_table, owner_count // block_count, axis=0)
    selector = selector3.reshape(owner_count * CAP, request_count)
    outgoing = jnp.einsum(
        "ocr,rd->ocd",
        selector3.astype(jnp.bfloat16),
        scaled.astype(jnp.bfloat16),
        preferred_element_type=jnp.float32,
    ).astype(jnp.bfloat16)
    incoming_half = lax.all_to_all(outgoing, "rows", split_axis=0, concat_axis=0, tiled=True)
    incoming = join_halves(incoming_half.reshape(owner_count * CAP, -1), myself)
    kept, given = swiglu_halves(incoming, cold_gate, cold_up, cold_down, myself)
    owner_sum = (kept + partner(given, "heads", 0)).astype(jnp.bfloat16)
    normed_late, owner_sum = lax.optimization_barrier((normed, owner_sum))
    returned = lax.all_to_all(
        owner_sum.reshape(owner_count, CAP, -1), "rows", split_axis=0, concat_axis=0, tiled=True
    )
    hot_kept, hot_given = swiglu_halves(normed_late, hot_gate, hot_up, hot_down, myself)
    hot_total = hot_kept + partner(hot_given, "heads", 0)
    cold_sum = collect_rows(
        selector.astype(jnp.float32),
        returned.reshape(owner_count * CAP, -1).astype(jnp.float32),
    )
    result = stream.astype(jnp.float32) + hot_total + cold_sum
    return result.astype(jnp.bfloat16)


def solution(mesh):
    return jax.shard_map(
        local,
        mesh=mesh,
        in_specs=(
            P(("groups", "rows"), "heads"),
            P(("groups", "rows"), "heads"),
            P(("groups", "rows"), "heads", None, None),
            P(("groups", "rows"), "heads", None, None),
            P(("groups", "rows"), "heads", None),
            P(("groups", "rows"), "heads", None),
            P(("groups", "rows")),
            P(),
            P("heads", None),
            P("heads", None),
            P("heads", None),
            P(("rows", "heads"), None),
            P(("rows", "heads"), None),
            P(("rows", "heads"), None),
            P(("groups", "rows"), None),
        ),
        out_specs=P(("groups", "rows"), "heads"),
        check_vma=False,
    )
```

```python
import jax
import jax.numpy as jnp
from jax import lax
from jax.sharding import PartitionSpec as P

HD = 128
D = 8192
CAP = 2


def partner(block, axis, bit):
    count = lax.axis_size(axis)
    route = []
    for low in range(count):
        high = low | 1 << bit
        if high != low and high < count:
            route += [(low, high), (high, low)]
    return lax.ppermute(block, axis, route)


def join_halves(half, myself):
    other = partner(half, "heads", 0)
    low_first = jnp.concatenate([half, other], axis=1)
    high_first = jnp.concatenate([other, half], axis=1)
    return jnp.where(myself == 0, low_first, high_first)


def attention_rows(query, key_cache, value_cache, key_new, value_new, lengths):
    count = key_cache.shape[0]
    kv_local = key_cache.shape[1]
    slots = key_cache.shape[2]
    scale_factor = 1.0 / HD**0.5
    queries = query.reshape(count, kv_local, -1, HD)
    keys_all = jnp.concatenate([key_cache, key_new[:, :, None, :]], axis=2)
    values_all = jnp.concatenate([value_cache, value_new[:, :, None, :]], axis=2)
    scores = (
        jnp.einsum("rgjd,rgpd->rgjp", queries, keys_all, preferred_element_type=jnp.float32)
        * scale_factor
    )
    positions = jnp.arange(slots + 1, dtype=jnp.int32)[None, :]
    visible = ((positions < lengths[:, None]) | (positions == slots))[:, None, None, :]
    scores = jnp.where(visible, scores, -1e30)
    highest = jnp.max(scores, axis=-1)
    expons = jnp.where(visible, jnp.exp(scores - highest[..., None]), 0.0)
    totals = jnp.sum(expons, axis=-1)
    weights = (expons / totals[..., None]).astype(jnp.bfloat16)
    blended = jnp.einsum(
        "rgjp,rgpd->rgjd", weights, values_all, preferred_element_type=jnp.float32
    )
    return blended.reshape(count, -1)


def swiglu_rows(normed, gate_rows, up_rows, down_rows):
    gate = jnp.einsum("rd,nd->rn", normed, gate_rows, preferred_element_type=jnp.float32)
    upper = jnp.einsum("rd,nd->rn", normed, up_rows, preferred_element_type=jnp.float32)
    hidden = (jax.nn.silu(gate) * upper).astype(jnp.bfloat16)
    return jnp.dot(hidden, down_rows, preferred_element_type=jnp.float32)


def swiglu_halves(normed, gate_rows, up_rows, down_rows, myself, rows_shape):
    gate = jnp.einsum("rd,nd->rn", normed, gate_rows, preferred_element_type=jnp.float32)
    upper = jnp.einsum("rd,nd->rn", normed, up_rows, preferred_element_type=jnp.float32)
    hidden = (jax.nn.silu(gate) * upper).astype(jnp.bfloat16)
    hidden = hidden.reshape(rows_shape + hidden.shape[-1:])
    half_width = down_rows.shape[1] // 2
    down_given = lax.dynamic_slice_in_dim(down_rows, (1 - myself) * half_width, half_width, 1)
    down_kept = lax.dynamic_slice_in_dim(down_rows, myself * half_width, half_width, 1)
    given = jnp.einsum("...n,nd->...d", hidden, down_given, preferred_element_type=jnp.float32)
    kept = jnp.einsum("...n,nd->...d", hidden, down_kept, preferred_element_type=jnp.float32)
    return kept, given


def collect_rows(selector, returned):
    return lax.dot_general(
        selector,
        returned,
        (((0,), (0,)), ((), ())),
        precision=lax.Precision.HIGHEST,
        preferred_element_type=jnp.float32,
    )


def local(
    residual_in,
    query,
    key_cache,
    value_cache,
    key_new,
    value_new,
    lengths,
    norm_gain,
    hot_gate,
    hot_up,
    hot_down,
    cold_gate,
    cold_up,
    cold_down,
    active,
):
    attended = attention_rows(query, key_cache, value_cache, key_new, value_new, lengths)
    stream = (residual_in.astype(jnp.float32) + attended).astype(jnp.bfloat16)
    half_width = stream.shape[1]
    myself = lax.axis_index("heads")
    local_wide = stream.astype(jnp.float32)
    square_part = jnp.sum(local_wide * local_wide, axis=-1)
    square_total = square_part + partner(square_part, "heads", 0)
    gain_half = lax.dynamic_slice_in_dim(norm_gain, myself * half_width, half_width)
    scaled = (
        local_wide * lax.rsqrt(square_total / D + 1e-05)[:, None] * gain_half.astype(jnp.float32)
    )
    normed = join_halves(scaled.astype(jnp.bfloat16), myself)
    owner_count = lax.axis_size("rows")
    block_count = active.shape[1]
    request_count = active.shape[0]
    by_block = jnp.transpose(active)
    earlier = jnp.cumsum(by_block, axis=1) - by_block
    slot_ids = jnp.arange(CAP, dtype=jnp.int32)[None, :, None]
    slot_table = by_block[:, None, :] * (earlier[:, None, :] == slot_ids).astype(jnp.int32)
    selector3 = jnp.repeat(slot_table, owner_count // block_count, axis=0)
    selector = selector3.reshape(owner_count * CAP, request_count)
    outgoing = jnp.einsum(
        "ocr,rd->ocd",
        selector3.astype(jnp.bfloat16),
        scaled.astype(jnp.bfloat16),
        preferred_element_type=jnp.float32,
    ).astype(jnp.bfloat16)
    incoming_half = lax.all_to_all(outgoing, "rows", split_axis=0, concat_axis=0, tiled=True)
    incoming = join_halves(incoming_half.reshape(owner_count * CAP, -1), myself)
    kept, given = swiglu_halves(
        incoming, cold_gate, cold_up, cold_down, myself, (owner_count, CAP)
    )
    owner_sum = (kept + partner(given, "heads", 0)).astype(jnp.bfloat16)
    normed_late, owner_sum = lax.optimization_barrier((normed, owner_sum))
    returned = lax.all_to_all(owner_sum, "rows", split_axis=0, concat_axis=0, tiled=True)
    hot_kept, hot_given = swiglu_halves(
        normed_late, hot_gate, hot_up, hot_down, myself, (request_count,)
    )
    hot_total = hot_kept + partner(hot_given, "heads", 0)
    cold_sum = collect_rows(
        selector.astype(jnp.float32),
        returned.reshape(owner_count * CAP, -1).astype(jnp.float32),
    )
    result = stream.astype(jnp.float32) + hot_total + cold_sum
    return result.astype(jnp.bfloat16)


def solution(mesh):
    return jax.shard_map(
        local,
        mesh=mesh,
        in_specs=(
            P(("groups", "rows"), "heads"),
            P(("groups", "rows"), "heads"),
            P(("groups", "rows"), "heads", None, None),
            P(("groups", "rows"), "heads", None, None),
            P(("groups", "rows"), "heads", None),
            P(("groups", "rows"), "heads", None),
            P(("groups", "rows")),
            P(),
            P("heads", None),
            P("heads", None),
            P("heads", None),
            P(("rows", "heads"), None),
            P(("rows", "heads"), None),
            P(("rows", "heads"), None),
            P(("groups", "rows"), None),
        ),
        out_specs=P(("groups", "rows"), "heads"),
        check_vma=False,
    )
```

```python
import jax
import jax.numpy as jnp
from jax import lax
from jax.sharding import PartitionSpec as P

HD = 128
D = 8192
CAP = 2


def partner(block, axis, bit):
    count = lax.axis_size(axis)
    route = []
    for low in range(count):
        high = low | 1 << bit
        if high != low and high < count:
            route += [(low, high), (high, low)]
    return lax.ppermute(block, axis, route)


def join_halves(half, myself):
    other = partner(half, "heads", 0)
    low_first = jnp.concatenate([half, other], axis=1)
    high_first = jnp.concatenate([other, half], axis=1)
    return jnp.where(myself == 0, low_first, high_first)


def attention_rows(query, key_cache, value_cache, key_new, value_new, lengths):
    count = key_cache.shape[0]
    kv_local = key_cache.shape[1]
    slots = key_cache.shape[2]
    scale_factor = 1.0 / HD**0.5
    queries = query.reshape(count, kv_local, -1, HD)
    keys_all = jnp.concatenate([key_cache, key_new[:, :, None, :]], axis=2)
    values_all = jnp.concatenate([value_cache, value_new[:, :, None, :]], axis=2)
    scores = (
        jnp.einsum("rgjd,rgpd->rgjp", queries, keys_all, preferred_element_type=jnp.float32)
        * scale_factor
    )
    positions = jnp.arange(slots + 1, dtype=jnp.int32)[None, :]
    visible = ((positions < lengths[:, None]) | (positions == slots))[:, None, None, :]
    scores = jnp.where(visible, scores, -1e30)
    highest = jnp.max(scores, axis=-1)
    expons = jnp.where(visible, jnp.exp(scores - highest[..., None]), 0.0)
    totals = jnp.sum(expons, axis=-1)
    weights = (expons / totals[..., None]).astype(jnp.bfloat16)
    blended = jnp.einsum(
        "rgjp,rgpd->rgjd", weights, values_all, preferred_element_type=jnp.float32
    )
    return blended.reshape(count, -1)


def swiglu_rows(normed, gate_rows, up_rows, down_rows):
    gate = jnp.einsum("rd,nd->rn", normed, gate_rows, preferred_element_type=jnp.float32)
    upper = jnp.einsum("rd,nd->rn", normed, up_rows, preferred_element_type=jnp.float32)
    hidden = (jax.nn.silu(gate) * upper).astype(jnp.bfloat16)
    return jnp.dot(hidden, down_rows, preferred_element_type=jnp.float32)


def swiglu_halves(normed, gate_rows, up_rows, down_rows, myself, rows_shape):
    gate = jnp.einsum("rd,nd->rn", normed, gate_rows, preferred_element_type=jnp.float32)
    upper = jnp.einsum("rd,nd->rn", normed, up_rows, preferred_element_type=jnp.float32)
    hidden = (jax.nn.silu(gate) * upper).astype(jnp.bfloat16)
    hidden = hidden.reshape(rows_shape + hidden.shape[-1:])
    half_width = down_rows.shape[1] // 2
    down_given = lax.dynamic_slice_in_dim(down_rows, (1 - myself) * half_width, half_width, 1)
    down_kept = lax.dynamic_slice_in_dim(down_rows, myself * half_width, half_width, 1)
    given = jnp.einsum("...n,nd->...d", hidden, down_given, preferred_element_type=jnp.float32)
    kept = jnp.einsum("...n,nd->...d", hidden, down_kept, preferred_element_type=jnp.float32)
    return kept, given


def collect_rows(selector, returned):
    return lax.dot_general(
        selector,
        returned,
        (((0,), (0,)), ((), ())),
        precision=lax.Precision.HIGHEST,
        preferred_element_type=jnp.float32,
    )


def local(
    residual_in,
    query,
    key_cache,
    value_cache,
    key_new,
    value_new,
    lengths,
    norm_gain,
    hot_gate,
    hot_up,
    hot_down,
    cold_gate,
    cold_up,
    cold_down,
    active,
):
    attended = attention_rows(query, key_cache, value_cache, key_new, value_new, lengths)
    stream = (residual_in.astype(jnp.float32) + attended).astype(jnp.bfloat16)
    half_width = stream.shape[1]
    myself = lax.axis_index("heads")
    local_wide = stream.astype(jnp.float32)
    square_part = jnp.sum(local_wide * local_wide, axis=-1)
    square_total = square_part + partner(square_part, "heads", 0)
    gain_half = lax.dynamic_slice_in_dim(norm_gain, myself * half_width, half_width)
    scaled = (
        local_wide * lax.rsqrt(square_total / D + 1e-05)[:, None] * gain_half.astype(jnp.float32)
    )
    owner_count = lax.axis_size("rows")
    block_count = active.shape[1]
    request_count = active.shape[0]
    by_block = jnp.transpose(active)
    earlier = jnp.cumsum(by_block, axis=1) - by_block
    slot_ids = jnp.arange(CAP, dtype=jnp.int32)[None, :, None]
    slot_table = by_block[:, None, :] * (earlier[:, None, :] == slot_ids).astype(jnp.int32)
    selector3 = jnp.repeat(slot_table, owner_count // block_count, axis=0)
    selector = selector3.reshape(owner_count * CAP, request_count)
    outgoing = jnp.einsum(
        "ocr,rd->ocd",
        selector3.astype(jnp.bfloat16),
        scaled.astype(jnp.bfloat16),
        preferred_element_type=jnp.float32,
    ).astype(jnp.bfloat16)
    incoming_half = lax.all_to_all(outgoing, "rows", split_axis=0, concat_axis=0, tiled=True)
    incoming = join_halves(incoming_half.reshape(owner_count * CAP, -1), myself)
    kept, given = swiglu_halves(
        incoming, cold_gate, cold_up, cold_down, myself, (owner_count, CAP)
    )
    owner_sum = (kept + partner(given, "heads", 0)).astype(jnp.bfloat16)
    scaled_late, owner_sum = lax.optimization_barrier((scaled.astype(jnp.bfloat16), owner_sum))
    normed_late = join_halves(scaled_late, myself)
    returned = lax.all_to_all(owner_sum, "rows", split_axis=0, concat_axis=0, tiled=True)
    hot_kept, hot_given = swiglu_halves(
        normed_late, hot_gate, hot_up, hot_down, myself, (request_count,)
    )
    hot_total = hot_kept + partner(hot_given, "heads", 0)
    cold_sum = collect_rows(
        selector.astype(jnp.float32),
        returned.reshape(owner_count * CAP, -1).astype(jnp.float32),
    )
    result = stream.astype(jnp.float32) + hot_total + cold_sum
    return result.astype(jnp.bfloat16)


def solution(mesh):
    return jax.shard_map(
        local,
        mesh=mesh,
        in_specs=(
            P(("groups", "rows"), "heads"),
            P(("groups", "rows"), "heads"),
            P(("groups", "rows"), "heads", None, None),
            P(("groups", "rows"), "heads", None, None),
            P(("groups", "rows"), "heads", None),
            P(("groups", "rows"), "heads", None),
            P(("groups", "rows")),
            P(),
            P("heads", None),
            P("heads", None),
            P("heads", None),
            P(("rows", "heads"), None),
            P(("rows", "heads"), None),
            P(("rows", "heads"), None),
            P(("groups", "rows"), None),
        ),
        out_specs=P(("groups", "rows"), "heads"),
        check_vma=False,
    )
```

```python
import jax
import jax.numpy as jnp
from jax import lax
from jax.sharding import PartitionSpec as P

HD = 128
D = 8192
CAP = 2


def partner(block, axis, bit):
    count = lax.axis_size(axis)
    route = []
    for low in range(count):
        high = low | 1 << bit
        if high != low and high < count:
            route += [(low, high), (high, low)]
    return lax.ppermute(block, axis, route)


def join_halves(half, myself):
    other = partner(half, "heads", 0)
    low_first = jnp.concatenate([half, other], axis=1)
    high_first = jnp.concatenate([other, half], axis=1)
    return jnp.where(myself == 0, low_first, high_first)


def attention_rows(query, key_cache, value_cache, key_new, value_new, lengths):
    count = key_cache.shape[0]
    kv_local = key_cache.shape[1]
    slots = key_cache.shape[2]
    scale_factor = 1.0 / HD**0.5
    queries = query.reshape(count, kv_local, -1, HD)
    keys_all = jnp.concatenate([key_cache, key_new[:, :, None, :]], axis=2)
    values_all = jnp.concatenate([value_cache, value_new[:, :, None, :]], axis=2)
    scores = (
        jnp.einsum("rgjd,rgpd->rgjp", queries, keys_all, preferred_element_type=jnp.float32)
        * scale_factor
    )
    positions = jnp.arange(slots + 1, dtype=jnp.int32)[None, :]
    visible = ((positions < lengths[:, None]) | (positions == slots))[:, None, None, :]
    scores = jnp.where(visible, scores, -1e30)
    highest = jnp.max(scores, axis=-1)
    expons = jnp.where(visible, jnp.exp(scores - highest[..., None]), 0.0)
    totals = jnp.sum(expons, axis=-1)
    weights = (expons / totals[..., None]).astype(jnp.bfloat16)
    blended = jnp.einsum(
        "rgjp,rgpd->rgjd", weights, values_all, preferred_element_type=jnp.float32
    )
    return blended.reshape(count, -1)


def swiglu_rows(normed, gate_rows, up_rows, down_rows):
    gate = jnp.einsum("rd,nd->rn", normed, gate_rows, preferred_element_type=jnp.float32)
    upper = jnp.einsum("rd,nd->rn", normed, up_rows, preferred_element_type=jnp.float32)
    hidden = (jax.nn.silu(gate) * upper).astype(jnp.bfloat16)
    return jnp.dot(hidden, down_rows, preferred_element_type=jnp.float32)


def swiglu_halves(normed, gate_rows, up_rows, down_rows, myself, rows_shape):
    gate = jnp.einsum("rd,nd->rn", normed, gate_rows, preferred_element_type=jnp.float32)
    upper = jnp.einsum("rd,nd->rn", normed, up_rows, preferred_element_type=jnp.float32)
    hidden = (jax.nn.silu(gate) * upper).astype(jnp.bfloat16)
    hidden = hidden.reshape(rows_shape + hidden.shape[-1:])
    half_width = down_rows.shape[1] // 2
    down_given = lax.dynamic_slice_in_dim(down_rows, (1 - myself) * half_width, half_width, 1)
    down_kept = lax.dynamic_slice_in_dim(down_rows, myself * half_width, half_width, 1)
    given = jnp.einsum("...n,nd->...d", hidden, down_given, preferred_element_type=jnp.float32)
    kept = jnp.einsum("...n,nd->...d", hidden, down_kept, preferred_element_type=jnp.float32)
    return kept, given


def cold_split(features, gate_rows, up_rows, myself):
    width = features.shape[1]
    gate_cols = lax.dynamic_slice_in_dim(gate_rows, myself * width, width, 1)
    up_cols = lax.dynamic_slice_in_dim(up_rows, myself * width, width, 1)
    gate = jnp.einsum("rd,nd->rn", features, gate_cols, preferred_element_type=jnp.float32)
    upper = jnp.einsum("rd,nd->rn", features, up_cols, preferred_element_type=jnp.float32)
    return [gate, upper]


def cold_down_half(gate, upper, down_rows, myself, rows_shape):
    hidden = (jax.nn.silu(gate) * upper).astype(jnp.bfloat16)
    hidden = hidden.reshape(rows_shape + hidden.shape[-1:])
    width = down_rows.shape[1] // 2
    down_cols = lax.dynamic_slice_in_dim(down_rows, myself * width, width, 1)
    return jnp.einsum("...n,nd->...d", hidden, down_cols, preferred_element_type=jnp.float32)


def collect_rows(selector, returned):
    return lax.dot_general(
        selector,
        returned,
        (((0,), (0,)), ((), ())),
        precision=lax.Precision.HIGHEST,
        preferred_element_type=jnp.float32,
    )


def local(
    residual_in,
    query,
    key_cache,
    value_cache,
    key_new,
    value_new,
    lengths,
    norm_gain,
    hot_gate,
    hot_up,
    hot_down,
    cold_gate,
    cold_up,
    cold_down,
    active,
):
    gate_other = partner(cold_gate, "heads", 0)
    up_other = partner(cold_up, "heads", 0)
    down_other = partner(cold_down, "heads", 0)
    attended = attention_rows(query, key_cache, value_cache, key_new, value_new, lengths)
    stream = (residual_in.astype(jnp.float32) + attended).astype(jnp.bfloat16)
    half_width = stream.shape[1]
    myself = lax.axis_index("heads")
    local_wide = stream.astype(jnp.float32)
    square_part = jnp.sum(local_wide * local_wide, axis=-1)
    square_total = square_part + partner(square_part, "heads", 0)
    gain_half = lax.dynamic_slice_in_dim(norm_gain, myself * half_width, half_width)
    scaled = (
        local_wide * lax.rsqrt(square_total / D + 1e-05)[:, None] * gain_half.astype(jnp.float32)
    )
    owner_count = lax.axis_size("rows")
    block_count = active.shape[1]
    request_count = active.shape[0]
    by_block = jnp.transpose(active)
    earlier = jnp.cumsum(by_block, axis=1) - by_block
    slot_ids = jnp.arange(CAP, dtype=jnp.int32)[None, :, None]
    slot_table = by_block[:, None, :] * (earlier[:, None, :] == slot_ids).astype(jnp.int32)
    selector3 = jnp.repeat(slot_table, owner_count // block_count, axis=0)
    selector = selector3.reshape(owner_count * CAP, request_count)
    outgoing = jnp.einsum(
        "ocr,rd->ocd",
        selector3.astype(jnp.bfloat16),
        scaled.astype(jnp.bfloat16),
        preferred_element_type=jnp.float32,
    ).astype(jnp.bfloat16)
    incoming_half = lax.all_to_all(outgoing, "rows", split_axis=0, concat_axis=0, tiled=True)
    features = incoming_half.reshape(owner_count * CAP, -1)
    mine = cold_split(features, cold_gate, cold_up, myself)
    theirs = cold_split(features, gate_other, up_other, myself)
    partials = jnp.stack(mine + theirs)
    echoed = partner(partials, "heads", 0)
    gate_mine = partials[0] + echoed[2]
    upper_mine = partials[1] + echoed[3]
    gate_theirs = partials[2] + echoed[0]
    upper_theirs = partials[3] + echoed[1]
    kept = cold_down_half(gate_mine, upper_mine, cold_down, myself, (owner_count, CAP))
    given = cold_down_half(gate_theirs, upper_theirs, down_other, myself, (owner_count, CAP))
    owner_sum = (kept + given).astype(jnp.bfloat16)
    scaled_late, owner_sum = lax.optimization_barrier((scaled.astype(jnp.bfloat16), owner_sum))
    normed_late = join_halves(scaled_late, myself)
    returned = lax.all_to_all(owner_sum, "rows", split_axis=0, concat_axis=0, tiled=True)
    hot_kept, hot_given = swiglu_halves(
        normed_late, hot_gate, hot_up, hot_down, myself, (request_count,)
    )
    hot_total = hot_kept + partner(hot_given, "heads", 0)
    cold_sum = collect_rows(
        selector.astype(jnp.float32),
        returned.reshape(owner_count * CAP, -1).astype(jnp.float32),
    )
    result = stream.astype(jnp.float32) + hot_total + cold_sum
    return result.astype(jnp.bfloat16)


def solution(mesh):
    return jax.shard_map(
        local,
        mesh=mesh,
        in_specs=(
            P(("groups", "rows"), "heads"),
            P(("groups", "rows"), "heads"),
            P(("groups", "rows"), "heads", None, None),
            P(("groups", "rows"), "heads", None, None),
            P(("groups", "rows"), "heads", None),
            P(("groups", "rows"), "heads", None),
            P(("groups", "rows")),
            P(),
            P("heads", None),
            P("heads", None),
            P("heads", None),
            P(("rows", "heads"), None),
            P(("rows", "heads"), None),
            P(("rows", "heads"), None),
            P(("groups", "rows"), None),
        ),
        out_specs=P(("groups", "rows"), "heads"),
        check_vma=False,
    )
```

```python
import jax
import jax.numpy as jnp
from jax import lax
from jax.sharding import PartitionSpec as P

HD = 128
D = 8192
CAP = 2


def partner(block, axis, bit):
    count = lax.axis_size(axis)
    route = []
    for low in range(count):
        high = low | 1 << bit
        if high != low and high < count:
            route += [(low, high), (high, low)]
    return lax.ppermute(block, axis, route)


def join_halves(half, myself):
    other = partner(half, "heads", 0)
    low_first = jnp.concatenate([half, other], axis=1)
    high_first = jnp.concatenate([other, half], axis=1)
    return jnp.where(myself == 0, low_first, high_first)


def attention_rows(query, key_cache, value_cache, key_new, value_new, lengths):
    count = key_cache.shape[0]
    kv_local = key_cache.shape[1]
    slots = key_cache.shape[2]
    scale_factor = 1.0 / HD**0.5
    queries = query.reshape(count, kv_local, -1, HD)
    keys_all = jnp.concatenate([key_cache, key_new[:, :, None, :]], axis=2)
    values_all = jnp.concatenate([value_cache, value_new[:, :, None, :]], axis=2)
    scores = (
        jnp.einsum("rgjd,rgpd->rgjp", queries, keys_all, preferred_element_type=jnp.float32)
        * scale_factor
    )
    positions = jnp.arange(slots + 1, dtype=jnp.int32)[None, :]
    visible = ((positions < lengths[:, None]) | (positions == slots))[:, None, None, :]
    scores = jnp.where(visible, scores, -1e30)
    highest = jnp.max(scores, axis=-1)
    expons = jnp.where(visible, jnp.exp(scores - highest[..., None]), 0.0)
    totals = jnp.sum(expons, axis=-1)
    weights = (expons / totals[..., None]).astype(jnp.bfloat16)
    blended = jnp.einsum(
        "rgjp,rgpd->rgjd", weights, values_all, preferred_element_type=jnp.float32
    )
    return blended.reshape(count, -1)


def swiglu_rows(normed, gate_rows, up_rows, down_rows):
    gate = jnp.einsum("rd,nd->rn", normed, gate_rows, preferred_element_type=jnp.float32)
    upper = jnp.einsum("rd,nd->rn", normed, up_rows, preferred_element_type=jnp.float32)
    hidden = (jax.nn.silu(gate) * upper).astype(jnp.bfloat16)
    return jnp.dot(hidden, down_rows, preferred_element_type=jnp.float32)


def swiglu_halves(normed, gate_rows, up_rows, down_rows, myself, rows_shape):
    gate = jnp.einsum("rd,nd->rn", normed, gate_rows, preferred_element_type=jnp.float32)
    upper = jnp.einsum("rd,nd->rn", normed, up_rows, preferred_element_type=jnp.float32)
    hidden = (jax.nn.silu(gate) * upper).astype(jnp.bfloat16)
    hidden = hidden.reshape(rows_shape + hidden.shape[-1:])
    half_width = down_rows.shape[1] // 2
    down_given = lax.dynamic_slice_in_dim(down_rows, (1 - myself) * half_width, half_width, 1)
    down_kept = lax.dynamic_slice_in_dim(down_rows, myself * half_width, half_width, 1)
    given = jnp.einsum("...n,nd->...d", hidden, down_given, preferred_element_type=jnp.float32)
    kept = jnp.einsum("...n,nd->...d", hidden, down_kept, preferred_element_type=jnp.float32)
    return kept, given


def my_half(rows, myself):
    width = rows.shape[1] // 2
    return lax.dynamic_slice_in_dim(rows, myself * width, width, 1)


def their_half(rows, myself):
    width = rows.shape[1] // 2
    return lax.dynamic_slice_in_dim(rows, (1 - myself) * width, width, 1)


def cold_split(features, gate_cols, up_cols):
    gate = jnp.einsum("rd,nd->rn", features, gate_cols, preferred_element_type=jnp.float32)
    upper = jnp.einsum("rd,nd->rn", features, up_cols, preferred_element_type=jnp.float32)
    return [gate, upper]


def cold_down_half(gate, upper, down_cols, rows_shape):
    hidden = (jax.nn.silu(gate) * upper).astype(jnp.bfloat16)
    hidden = hidden.reshape(rows_shape + hidden.shape[-1:])
    return jnp.einsum("...n,nd->...d", hidden, down_cols, preferred_element_type=jnp.float32)


def collect_rows(selector, returned):
    return lax.dot_general(
        selector,
        returned,
        (((0,), (0,)), ((), ())),
        precision=lax.Precision.HIGHEST,
        preferred_element_type=jnp.float32,
    )


def local(
    residual_in,
    query,
    key_cache,
    value_cache,
    key_new,
    value_new,
    lengths,
    norm_gain,
    hot_gate,
    hot_up,
    hot_down,
    cold_gate,
    cold_up,
    cold_down,
    active,
):
    myself = lax.axis_index("heads")
    gate_other = partner(their_half(cold_gate, myself), "heads", 0)
    up_other = partner(their_half(cold_up, myself), "heads", 0)
    down_other = partner(their_half(cold_down, myself), "heads", 0)
    attended = attention_rows(query, key_cache, value_cache, key_new, value_new, lengths)
    stream = (residual_in.astype(jnp.float32) + attended).astype(jnp.bfloat16)
    half_width = stream.shape[1]
    myself = lax.axis_index("heads")
    local_wide = stream.astype(jnp.float32)
    square_part = jnp.sum(local_wide * local_wide, axis=-1)
    square_total = square_part + partner(square_part, "heads", 0)
    gain_half = lax.dynamic_slice_in_dim(norm_gain, myself * half_width, half_width)
    scaled = (
        local_wide * lax.rsqrt(square_total / D + 1e-05)[:, None] * gain_half.astype(jnp.float32)
    )
    owner_count = lax.axis_size("rows")
    block_count = active.shape[1]
    request_count = active.shape[0]
    by_block = jnp.transpose(active)
    earlier = jnp.cumsum(by_block, axis=1) - by_block
    slot_ids = jnp.arange(CAP, dtype=jnp.int32)[None, :, None]
    slot_table = by_block[:, None, :] * (earlier[:, None, :] == slot_ids).astype(jnp.int32)
    selector3 = jnp.repeat(slot_table, owner_count // block_count, axis=0)
    selector = selector3.reshape(owner_count * CAP, request_count)
    outgoing = jnp.einsum(
        "ocr,rd->ocd",
        selector3.astype(jnp.bfloat16),
        scaled.astype(jnp.bfloat16),
        preferred_element_type=jnp.float32,
    ).astype(jnp.bfloat16)
    incoming_half = lax.all_to_all(outgoing, "rows", split_axis=0, concat_axis=0, tiled=True)
    features, gate_other, up_other, down_other = lax.optimization_barrier(
        (incoming_half.reshape(owner_count * CAP, -1), gate_other, up_other, down_other)
    )
    mine = cold_split(features, my_half(cold_gate, myself), my_half(cold_up, myself))
    theirs = cold_split(features, gate_other, up_other)
    partials = jnp.stack(mine + theirs)
    echoed = partner(partials, "heads", 0)
    gate_mine = partials[0] + echoed[2]
    upper_mine = partials[1] + echoed[3]
    gate_theirs = partials[2] + echoed[0]
    upper_theirs = partials[3] + echoed[1]
    kept = cold_down_half(gate_mine, upper_mine, my_half(cold_down, myself), (owner_count, CAP))
    given = cold_down_half(gate_theirs, upper_theirs, down_other, (owner_count, CAP))
    owner_sum = (kept + given).astype(jnp.bfloat16)
    scaled_late, owner_sum = lax.optimization_barrier((scaled.astype(jnp.bfloat16), owner_sum))
    normed_late = join_halves(scaled_late, myself)
    returned = lax.all_to_all(owner_sum, "rows", split_axis=0, concat_axis=0, tiled=True)
    hot_kept, hot_given = swiglu_halves(
        normed_late, hot_gate, hot_up, hot_down, myself, (request_count,)
    )
    hot_total = hot_kept + partner(hot_given, "heads", 0)
    cold_sum = collect_rows(
        selector.astype(jnp.float32),
        returned.reshape(owner_count * CAP, -1).astype(jnp.float32),
    )
    result = stream.astype(jnp.float32) + hot_total + cold_sum
    return result.astype(jnp.bfloat16)


def solution(mesh):
    return jax.shard_map(
        local,
        mesh=mesh,
        in_specs=(
            P(("groups", "rows"), "heads"),
            P(("groups", "rows"), "heads"),
            P(("groups", "rows"), "heads", None, None),
            P(("groups", "rows"), "heads", None, None),
            P(("groups", "rows"), "heads", None),
            P(("groups", "rows"), "heads", None),
            P(("groups", "rows")),
            P(),
            P("heads", None),
            P("heads", None),
            P("heads", None),
            P(("rows", "heads"), None),
            P(("rows", "heads"), None),
            P(("rows", "heads"), None),
            P(("groups", "rows"), None),
        ),
        out_specs=P(("groups", "rows"), "heads"),
        check_vma=False,
    )
```

```python
import jax
import jax.numpy as jnp
from jax import lax
from jax.sharding import PartitionSpec as P

HD = 128
D = 8192
CAP = 2


def partner(block, axis, bit):
    count = lax.axis_size(axis)
    route = []
    for low in range(count):
        high = low | 1 << bit
        if high != low and high < count:
            route += [(low, high), (high, low)]
    return lax.ppermute(block, axis, route)


def join_halves(half, myself):
    other = partner(half, "heads", 0)
    low_first = jnp.concatenate([half, other], axis=1)
    high_first = jnp.concatenate([other, half], axis=1)
    return jnp.where(myself == 0, low_first, high_first)


def attention_rows(query, key_cache, value_cache, key_new, value_new, lengths):
    count = key_cache.shape[0]
    kv_local = key_cache.shape[1]
    slots = key_cache.shape[2]
    scale_factor = 1.0 / HD**0.5
    queries = query.reshape(count, kv_local, -1, HD)
    keys_all = jnp.concatenate([key_cache, key_new[:, :, None, :]], axis=2)
    values_all = jnp.concatenate([value_cache, value_new[:, :, None, :]], axis=2)
    scores = (
        jnp.einsum("rgjd,rgpd->rgjp", queries, keys_all, preferred_element_type=jnp.float32)
        * scale_factor
    )
    positions = jnp.arange(slots + 1, dtype=jnp.int32)[None, :]
    visible = ((positions < lengths[:, None]) | (positions == slots))[:, None, None, :]
    scores = jnp.where(visible, scores, -1e30)
    highest = jnp.max(scores, axis=-1)
    expons = jnp.where(visible, jnp.exp(scores - highest[..., None]), 0.0)
    totals = jnp.sum(expons, axis=-1)
    weights = (expons / totals[..., None]).astype(jnp.bfloat16)
    blended = jnp.einsum(
        "rgjp,rgpd->rgjd", weights, values_all, preferred_element_type=jnp.float32
    )
    return blended.reshape(count, -1)


def swiglu_rows(normed, gate_rows, up_rows, down_rows):
    gate = jnp.einsum("rd,nd->rn", normed, gate_rows, preferred_element_type=jnp.float32)
    upper = jnp.einsum("rd,nd->rn", normed, up_rows, preferred_element_type=jnp.float32)
    hidden = (jax.nn.silu(gate) * upper).astype(jnp.bfloat16)
    return jnp.dot(hidden, down_rows, preferred_element_type=jnp.float32)


def swiglu_halves(normed, gate_rows, up_rows, down_rows, myself, rows_shape):
    gate = jnp.einsum("rd,nd->rn", normed, gate_rows, preferred_element_type=jnp.float32)
    upper = jnp.einsum("rd,nd->rn", normed, up_rows, preferred_element_type=jnp.float32)
    hidden = (jax.nn.silu(gate) * upper).astype(jnp.bfloat16)
    hidden = hidden.reshape(rows_shape + hidden.shape[-1:])
    half_width = down_rows.shape[1] // 2
    down_given = lax.dynamic_slice_in_dim(down_rows, (1 - myself) * half_width, half_width, 1)
    down_kept = lax.dynamic_slice_in_dim(down_rows, myself * half_width, half_width, 1)
    given = jnp.einsum("...n,nd->...d", hidden, down_given, preferred_element_type=jnp.float32)
    kept = jnp.einsum("...n,nd->...d", hidden, down_kept, preferred_element_type=jnp.float32)
    return kept, given


def collect_rows(selector, returned):
    return lax.dot_general(
        selector,
        returned,
        (((0,), (0,)), ((), ())),
        precision=lax.Precision.HIGHEST,
        preferred_element_type=jnp.float32,
    )


def local(
    residual_in,
    query,
    key_cache,
    value_cache,
    key_new,
    value_new,
    lengths,
    norm_gain,
    hot_gate,
    hot_up,
    hot_down,
    cold_gate,
    cold_up,
    cold_down,
    active,
):
    attended = attention_rows(query, key_cache, value_cache, key_new, value_new, lengths)
    stream = (residual_in.astype(jnp.float32) + attended).astype(jnp.bfloat16)
    half_width = stream.shape[1]
    myself = lax.axis_index("heads")
    local_wide = stream.astype(jnp.float32)
    square_part = jnp.sum(local_wide * local_wide, axis=-1)
    square_total = square_part + partner(square_part, "heads", 0)
    gain_half = lax.dynamic_slice_in_dim(norm_gain, myself * half_width, half_width)
    scaled = (
        local_wide * lax.rsqrt(square_total / D + 1e-05)[:, None] * gain_half.astype(jnp.float32)
    )
    normed = join_halves(scaled.astype(jnp.bfloat16), myself)
    owner_count = lax.axis_size("rows")
    block_count = active.shape[1]
    request_count = active.shape[0]
    by_block = jnp.transpose(active)
    earlier = jnp.cumsum(by_block, axis=1) - by_block
    slot_ids = jnp.arange(CAP, dtype=jnp.int32)[None, :, None]
    slot_table = by_block[:, None, :] * (earlier[:, None, :] == slot_ids).astype(jnp.int32)
    selector3 = jnp.repeat(slot_table, owner_count // block_count, axis=0)
    selector = selector3.reshape(owner_count * CAP, request_count)
    outgoing = jnp.einsum(
        "ocr,rd->ocd",
        selector3.astype(jnp.bfloat16),
        scaled.astype(jnp.bfloat16),
        preferred_element_type=jnp.float32,
    ).astype(jnp.bfloat16)
    incoming_half = lax.all_to_all(outgoing, "rows", split_axis=0, concat_axis=0, tiled=True)
    incoming = join_halves(incoming_half.reshape(owner_count * CAP, -1), myself)
    kept, given = swiglu_halves(
        incoming, cold_gate, cold_up, cold_down, myself, (owner_count, CAP)
    )
    given_narrow = partner(given.astype(jnp.bfloat16), "heads", 0)
    owner_sum = (kept + given_narrow.astype(jnp.float32)).astype(jnp.bfloat16)
    normed_late, owner_sum = lax.optimization_barrier((normed, owner_sum))
    returned = lax.all_to_all(owner_sum, "rows", split_axis=0, concat_axis=0, tiled=True)
    hot_kept, hot_given = swiglu_halves(
        normed_late, hot_gate, hot_up, hot_down, myself, (request_count,)
    )
    hot_total = hot_kept + partner(hot_given, "heads", 0)
    cold_sum = collect_rows(
        selector.astype(jnp.float32),
        returned.reshape(owner_count * CAP, -1).astype(jnp.float32),
    )
    result = stream.astype(jnp.float32) + hot_total + cold_sum
    return result.astype(jnp.bfloat16)


def solution(mesh):
    return jax.shard_map(
        local,
        mesh=mesh,
        in_specs=(
            P(("groups", "rows"), "heads"),
            P(("groups", "rows"), "heads"),
            P(("groups", "rows"), "heads", None, None),
            P(("groups", "rows"), "heads", None, None),
            P(("groups", "rows"), "heads", None),
            P(("groups", "rows"), "heads", None),
            P(("groups", "rows")),
            P(),
            P("heads", None),
            P("heads", None),
            P("heads", None),
            P(("rows", "heads"), None),
            P(("rows", "heads"), None),
            P(("rows", "heads"), None),
            P(("groups", "rows"), None),
        ),
        out_specs=P(("groups", "rows"), "heads"),
        check_vma=False,
    )
```

```python
import jax
import jax.numpy as jnp
from jax import lax
from jax.sharding import PartitionSpec as P
from jax.experimental.layout import Layout, with_layout_constraint

HD = 128
D = 8192
CAP = 2


def partner(block, axis, bit):
    count = lax.axis_size(axis)
    route = []
    for low in range(count):
        high = low | 1 << bit
        if high != low and high < count:
            route += [(low, high), (high, low)]
    return lax.ppermute(block, axis, route)


def join_halves(half, myself):
    other = partner(half, "heads", 0)
    low_first = jnp.concatenate([half, other], axis=1)
    high_first = jnp.concatenate([other, half], axis=1)
    return jnp.where(myself == 0, low_first, high_first)


def attention_rows(query, key_cache, value_cache, key_new, value_new, lengths):
    count = key_cache.shape[0]
    kv_local = key_cache.shape[1]
    slots = key_cache.shape[2]
    scale_factor = 1.0 / HD**0.5
    queries = query.reshape(count, kv_local, -1, HD)
    keys_all = jnp.concatenate([key_cache, key_new[:, :, None, :]], axis=2)
    values_all = jnp.concatenate([value_cache, value_new[:, :, None, :]], axis=2)
    scores = (
        jnp.einsum("rgjd,rgpd->rgjp", queries, keys_all, preferred_element_type=jnp.float32)
        * scale_factor
    )
    positions = jnp.arange(slots + 1, dtype=jnp.int32)[None, :]
    visible = ((positions < lengths[:, None]) | (positions == slots))[:, None, None, :]
    scores = jnp.where(visible, scores, -1e30)
    highest = jnp.max(scores, axis=-1)
    expons = jnp.where(visible, jnp.exp(scores - highest[..., None]), 0.0)
    totals = jnp.sum(expons, axis=-1)
    weights = (expons / totals[..., None]).astype(jnp.bfloat16)
    blended = jnp.einsum(
        "rgjp,rgpd->rgjd", weights, values_all, preferred_element_type=jnp.float32
    )
    return blended.reshape(count, -1)


def swiglu_rows(normed, gate_rows, up_rows, down_rows):
    gate = jnp.einsum("rd,nd->rn", normed, gate_rows, preferred_element_type=jnp.float32)
    upper = jnp.einsum("rd,nd->rn", normed, up_rows, preferred_element_type=jnp.float32)
    hidden = (jax.nn.silu(gate) * upper).astype(jnp.bfloat16)
    return jnp.dot(hidden, down_rows, preferred_element_type=jnp.float32)


def swiglu_halves(normed, gate_rows, up_rows, down_rows, myself, rows_shape):
    gate = jnp.einsum("rd,nd->rn", normed, gate_rows, preferred_element_type=jnp.float32)
    upper = jnp.einsum("rd,nd->rn", normed, up_rows, preferred_element_type=jnp.float32)
    hidden = (jax.nn.silu(gate) * upper).astype(jnp.bfloat16)
    hidden = hidden.reshape(rows_shape + hidden.shape[-1:])
    half_width = down_rows.shape[1] // 2
    down_given = lax.dynamic_slice_in_dim(down_rows, (1 - myself) * half_width, half_width, 1)
    down_kept = lax.dynamic_slice_in_dim(down_rows, myself * half_width, half_width, 1)
    given = jnp.einsum("...n,nd->...d", hidden, down_given, preferred_element_type=jnp.float32)
    kept = jnp.einsum("...n,nd->...d", hidden, down_kept, preferred_element_type=jnp.float32)
    return kept, given


def collect_rows(selector, returned):
    return lax.dot_general(
        selector,
        returned,
        (((0,), (0,)), ((), ())),
        precision=lax.Precision.HIGHEST,
        preferred_element_type=jnp.float32,
    )


def local(
    residual_in,
    query,
    key_cache,
    value_cache,
    key_new,
    value_new,
    lengths,
    norm_gain,
    hot_gate,
    hot_up,
    hot_down,
    cold_gate,
    cold_up,
    cold_down,
    active,
):
    attended = attention_rows(query, key_cache, value_cache, key_new, value_new, lengths)
    stream = (residual_in.astype(jnp.float32) + attended).astype(jnp.bfloat16)
    half_width = stream.shape[1]
    myself = lax.axis_index("heads")
    local_wide = stream.astype(jnp.float32)
    square_part = jnp.sum(local_wide * local_wide, axis=-1)
    square_total = square_part + partner(square_part, "heads", 0)
    gain_half = lax.dynamic_slice_in_dim(norm_gain, myself * half_width, half_width)
    scaled = (
        local_wide * lax.rsqrt(square_total / D + 1e-05)[:, None] * gain_half.astype(jnp.float32)
    )
    normed = join_halves(scaled.astype(jnp.bfloat16), myself)
    owner_count = lax.axis_size("rows")
    block_count = active.shape[1]
    request_count = active.shape[0]
    by_block = jnp.transpose(active)
    earlier = jnp.cumsum(by_block, axis=1) - by_block
    slot_ids = jnp.arange(CAP, dtype=jnp.int32)[None, :, None]
    slot_table = by_block[:, None, :] * (earlier[:, None, :] == slot_ids).astype(jnp.int32)
    selector3 = jnp.repeat(slot_table, owner_count // block_count, axis=0)
    selector = selector3.reshape(owner_count * CAP, request_count)
    outgoing = jnp.einsum(
        "ocr,rd->ocd",
        selector3.astype(jnp.bfloat16),
        scaled.astype(jnp.bfloat16),
        preferred_element_type=jnp.float32,
    ).astype(jnp.bfloat16)
    incoming_half = lax.all_to_all(outgoing, "rows", split_axis=0, concat_axis=0, tiled=True)
    incoming = join_halves(incoming_half.reshape(owner_count * CAP, -1), myself)
    kept, given = swiglu_halves(
        incoming, cold_gate, cold_up, cold_down, myself, (owner_count, CAP)
    )
    given_narrow = partner(given.astype(jnp.bfloat16), "heads", 0)
    owner_sum = (kept + given_narrow.astype(jnp.float32)).astype(jnp.bfloat16)
    owner_sum = with_layout_constraint(owner_sum, Layout((0, 1, 2)))
    normed_late, owner_sum = lax.optimization_barrier((normed, owner_sum))
    returned = lax.all_to_all(owner_sum, "rows", split_axis=0, concat_axis=0, tiled=True)
    hot_kept, hot_given = swiglu_halves(
        normed_late, hot_gate, hot_up, hot_down, myself, (request_count,)
    )
    hot_total = hot_kept + partner(hot_given, "heads", 0)
    cold_sum = collect_rows(
        selector.astype(jnp.float32),
        returned.reshape(owner_count * CAP, -1).astype(jnp.float32),
    )
    result = stream.astype(jnp.float32) + hot_total + cold_sum
    return result.astype(jnp.bfloat16)


def solution(mesh):
    return jax.shard_map(
        local,
        mesh=mesh,
        in_specs=(
            P(("groups", "rows"), "heads"),
            P(("groups", "rows"), "heads"),
            P(("groups", "rows"), "heads", None, None),
            P(("groups", "rows"), "heads", None, None),
            P(("groups", "rows"), "heads", None),
            P(("groups", "rows"), "heads", None),
            P(("groups", "rows")),
            P(),
            P("heads", None),
            P("heads", None),
            P("heads", None),
            P(("rows", "heads"), None),
            P(("rows", "heads"), None),
            P(("rows", "heads"), None),
            P(("groups", "rows"), None),
        ),
        out_specs=P(("groups", "rows"), "heads"),
        check_vma=False,
    )
```

```python
import jax
import jax.numpy as jnp
from jax import lax
from jax.sharding import PartitionSpec as P
from jax.experimental import pallas as pl
from jax.experimental.pallas import tpu as pltpu

HD = 128
D = 8192
CAP = 2


def partner(block, axis, bit):
    count = lax.axis_size(axis)
    route = []
    for low in range(count):
        high = low | 1 << bit
        if high != low and high < count:
            route += [(low, high), (high, low)]
    return lax.ppermute(block, axis, route)


def join_halves(half, myself):
    other = partner(half, "heads", 0)
    low_first = jnp.concatenate([half, other], axis=1)
    high_first = jnp.concatenate([other, half], axis=1)
    return jnp.where(myself == 0, low_first, high_first)


def attention_kernel(len_ref, q_ref, k_ref, v_ref, kn_ref, vn_ref, out_ref):
    count, groups, heads, _ = q_ref.shape
    slots = k_ref.shape[2]
    scale_factor = 1.0 / HD**0.5
    for r in range(count):
        length = len_ref[r]
        for g in range(groups):
            q = q_ref[r, g]
            k = k_ref[r, g]
            scores = (
                lax.dot_general(q, k, (((1,), (1,)), ((), ())), preferred_element_type=jnp.float32)
                * scale_factor
            )
            key_new = kn_ref[r, pl.ds(g, 1), :].astype(jnp.float32)
            own = jnp.sum(q.astype(jnp.float32) * key_new, axis=1, keepdims=True) * scale_factor
            visible = lax.broadcasted_iota(jnp.int32, (heads, slots), 1) < length
            scores = jnp.where(visible, scores, -1e30)
            highest = jnp.maximum(jnp.max(scores, axis=1, keepdims=True), own)
            expons = jnp.where(visible, jnp.exp(scores - highest), 0.0)
            own_expon = jnp.exp(own - highest)
            totals = jnp.sum(expons, axis=1, keepdims=True) + own_expon
            weights = (expons / totals).astype(jnp.bfloat16)
            own_weight = (own_expon / totals).astype(jnp.bfloat16).astype(jnp.float32)
            blended = jnp.dot(weights, v_ref[r, g], preferred_element_type=jnp.float32)
            value_new = vn_ref[r, pl.ds(g, 1), :].astype(jnp.float32)
            out_ref[r, g] = blended + own_weight * value_new


def attention_rows(query, key_cache, value_cache, key_new, value_new, lengths):
    count, kv_local, slots, _ = key_cache.shape
    queries = query.reshape(count, kv_local, -1, HD)
    vmem = pl.BlockSpec(memory_space=pltpu.VMEM)
    blended = pl.pallas_call(
        attention_kernel,
        out_shape=jax.ShapeDtypeStruct(queries.shape, jnp.float32),
        in_specs=[pl.BlockSpec(memory_space=pltpu.SMEM)] + [vmem] * 5,
        out_specs=vmem,
        cost_estimate=pl.CostEstimate(
            flops=4 * queries.size * slots, transcendentals=queries.size // HD * slots,
            bytes_accessed=2 * (queries.size + 2 * key_cache.size) + 4 * queries.size,
        ),
    )(lengths, queries, key_cache, value_cache, key_new, value_new)
    return blended.reshape(count, -1)


def swiglu_rows(normed, gate_rows, up_rows, down_rows):
    gate = jnp.einsum("rd,nd->rn", normed, gate_rows, preferred_element_type=jnp.float32)
    upper = jnp.einsum("rd,nd->rn", normed, up_rows, preferred_element_type=jnp.float32)
    hidden = (jax.nn.silu(gate) * upper).astype(jnp.bfloat16)
    return jnp.dot(hidden, down_rows, preferred_element_type=jnp.float32)


def swiglu_halves(normed, gate_rows, up_rows, down_rows, myself, rows_shape):
    gate = jnp.einsum("rd,nd->rn", normed, gate_rows, preferred_element_type=jnp.float32)
    upper = jnp.einsum("rd,nd->rn", normed, up_rows, preferred_element_type=jnp.float32)
    hidden = (jax.nn.silu(gate) * upper).astype(jnp.bfloat16)
    hidden = hidden.reshape(rows_shape + hidden.shape[-1:])
    half_width = down_rows.shape[1] // 2
    down_given = lax.dynamic_slice_in_dim(down_rows, (1 - myself) * half_width, half_width, 1)
    down_kept = lax.dynamic_slice_in_dim(down_rows, myself * half_width, half_width, 1)
    given = jnp.einsum("...n,nd->...d", hidden, down_given, preferred_element_type=jnp.float32)
    kept = jnp.einsum("...n,nd->...d", hidden, down_kept, preferred_element_type=jnp.float32)
    return kept, given


def collect_rows(selector, returned):
    return lax.dot_general(
        selector,
        returned,
        (((0,), (0,)), ((), ())),
        precision=lax.Precision.HIGHEST,
        preferred_element_type=jnp.float32,
    )


def local(
    residual_in,
    query,
    key_cache,
    value_cache,
    key_new,
    value_new,
    lengths,
    norm_gain,
    hot_gate,
    hot_up,
    hot_down,
    cold_gate,
    cold_up,
    cold_down,
    active,
):
    attended = attention_rows(query, key_cache, value_cache, key_new, value_new, lengths)
    stream = (residual_in.astype(jnp.float32) + attended).astype(jnp.bfloat16)
    half_width = stream.shape[1]
    myself = lax.axis_index("heads")
    local_wide = stream.astype(jnp.float32)
    square_part = jnp.sum(local_wide * local_wide, axis=-1)
    square_total = square_part + partner(square_part, "heads", 0)
    gain_half = lax.dynamic_slice_in_dim(norm_gain, myself * half_width, half_width)
    scaled = (
        local_wide * lax.rsqrt(square_total / D + 1e-05)[:, None] * gain_half.astype(jnp.float32)
    )
    normed = join_halves(scaled.astype(jnp.bfloat16), myself)
    owner_count = lax.axis_size("rows")
    block_count = active.shape[1]
    request_count = active.shape[0]
    by_block = jnp.transpose(active)
    earlier = jnp.cumsum(by_block, axis=1) - by_block
    slot_ids = jnp.arange(CAP, dtype=jnp.int32)[None, :, None]
    slot_table = by_block[:, None, :] * (earlier[:, None, :] == slot_ids).astype(jnp.int32)
    selector3 = jnp.repeat(slot_table, owner_count // block_count, axis=0)
    selector = selector3.reshape(owner_count * CAP, request_count)
    outgoing = jnp.einsum(
        "ocr,rd->ocd",
        selector3.astype(jnp.bfloat16),
        scaled.astype(jnp.bfloat16),
        preferred_element_type=jnp.float32,
    ).astype(jnp.bfloat16)
    incoming_half = lax.all_to_all(outgoing, "rows", split_axis=0, concat_axis=0, tiled=True)
    incoming = join_halves(incoming_half.reshape(owner_count * CAP, -1), myself)
    kept, given = swiglu_halves(
        incoming, cold_gate, cold_up, cold_down, myself, (owner_count, CAP)
    )
    given_narrow = partner(given.astype(jnp.bfloat16), "heads", 0)
    owner_sum = (kept + given_narrow.astype(jnp.float32)).astype(jnp.bfloat16)
    normed_late, owner_sum = lax.optimization_barrier((normed, owner_sum))
    returned = lax.all_to_all(owner_sum, "rows", split_axis=0, concat_axis=0, tiled=True)
    hot_kept, hot_given = swiglu_halves(
        normed_late, hot_gate, hot_up, hot_down, myself, (request_count,)
    )
    hot_total = hot_kept + partner(hot_given, "heads", 0)
    cold_sum = collect_rows(
        selector.astype(jnp.float32),
        returned.reshape(owner_count * CAP, -1).astype(jnp.float32),
    )
    result = stream.astype(jnp.float32) + hot_total + cold_sum
    return result.astype(jnp.bfloat16)


def solution(mesh):
    return jax.shard_map(
        local,
        mesh=mesh,
        in_specs=(
            P(("groups", "rows"), "heads"),
            P(("groups", "rows"), "heads"),
            P(("groups", "rows"), "heads", None, None),
            P(("groups", "rows"), "heads", None, None),
            P(("groups", "rows"), "heads", None),
            P(("groups", "rows"), "heads", None),
            P(("groups", "rows")),
            P(),
            P("heads", None),
            P("heads", None),
            P("heads", None),
            P(("rows", "heads"), None),
            P(("rows", "heads"), None),
            P(("rows", "heads"), None),
            P(("groups", "rows"), None),
        ),
        out_specs=P(("groups", "rows"), "heads"),
        check_vma=False,
    )
```

```python
import jax
import jax.numpy as jnp
from jax import lax
from jax.sharding import PartitionSpec as P

HD = 128
D = 8192
CAP = 2


def partner(block, axis, bit):
    count = lax.axis_size(axis)
    route = []
    for low in range(count):
        high = low | 1 << bit
        if high != low and high < count:
            route += [(low, high), (high, low)]
    return lax.ppermute(block, axis, route)


def join_halves(half, myself):
    other = partner(half, "heads", 0)
    low_first = jnp.concatenate([half, other], axis=1)
    high_first = jnp.concatenate([other, half], axis=1)
    return jnp.where(myself == 0, low_first, high_first)


def attention_rows(query, key_cache, value_cache, key_new, value_new, lengths):
    count = key_cache.shape[0]
    kv_local = key_cache.shape[1]
    slots = key_cache.shape[2]
    scale_factor = 1.0 / HD**0.5
    queries = query.reshape(count, kv_local, -1, HD)
    keys_all = jnp.concatenate([key_cache, key_new[:, :, None, :]], axis=2)
    values_all = jnp.concatenate([value_cache, value_new[:, :, None, :]], axis=2)
    scores = (
        jnp.einsum("rgjd,rgpd->rgjp", queries, keys_all, preferred_element_type=jnp.float32)
        * scale_factor
    )
    positions = jnp.arange(slots + 1, dtype=jnp.int32)[None, :]
    visible = ((positions < lengths[:, None]) | (positions == slots))[:, None, None, :]
    scores = jnp.where(visible, scores, -1e30)
    highest = jnp.max(scores, axis=-1)
    expons = jnp.where(visible, jnp.exp(scores - highest[..., None]), 0.0)
    totals = jnp.sum(expons, axis=-1)
    weights = (expons / totals[..., None]).astype(jnp.bfloat16)
    blended = jnp.einsum(
        "rgjp,rgpd->rgjd", weights, values_all, preferred_element_type=jnp.float32
    )
    return blended.reshape(count, -1)


def normalize_rows(rows, norm_gain):
    wide = rows.astype(jnp.float32)
    mean_square = jnp.sum(wide * wide, axis=-1, keepdims=True) / D
    scaled = wide * lax.rsqrt(mean_square + 1e-05) * norm_gain.astype(jnp.float32)
    return scaled.astype(jnp.bfloat16)


def swiglu_rows(normed, gate_rows, up_rows, down_rows):
    gate = jnp.einsum("rd,nd->rn", normed, gate_rows, preferred_element_type=jnp.float32)
    upper = jnp.einsum("rd,nd->rn", normed, up_rows, preferred_element_type=jnp.float32)
    hidden = (jax.nn.silu(gate) * upper).astype(jnp.bfloat16)
    return jnp.dot(hidden, down_rows, preferred_element_type=jnp.float32)


def swiglu_halves(normed, gate_rows, up_rows, down_rows, myself, rows_shape):
    gate = jnp.einsum("rd,nd->rn", normed, gate_rows, preferred_element_type=jnp.float32)
    upper = jnp.einsum("rd,nd->rn", normed, up_rows, preferred_element_type=jnp.float32)
    hidden = (jax.nn.silu(gate) * upper).astype(jnp.bfloat16)
    hidden = hidden.reshape(rows_shape + hidden.shape[-1:])
    half_width = down_rows.shape[1] // 2
    down_given = lax.dynamic_slice_in_dim(down_rows, (1 - myself) * half_width, half_width, 1)
    down_kept = lax.dynamic_slice_in_dim(down_rows, myself * half_width, half_width, 1)
    given = jnp.einsum("...n,nd->...d", hidden, down_given, preferred_element_type=jnp.float32)
    kept = jnp.einsum("...n,nd->...d", hidden, down_kept, preferred_element_type=jnp.float32)
    return kept, given


def collect_rows(selector, returned):
    return lax.dot_general(
        selector,
        returned,
        (((0,), (0,)), ((), ())),
        precision=lax.Precision.HIGHEST,
        preferred_element_type=jnp.float32,
    )


def local(
    residual_in,
    query,
    key_cache,
    value_cache,
    key_new,
    value_new,
    lengths,
    norm_gain,
    hot_gate,
    hot_up,
    hot_down,
    cold_gate,
    cold_up,
    cold_down,
    active,
):
    attended = attention_rows(query, key_cache, value_cache, key_new, value_new, lengths)
    stream = (residual_in.astype(jnp.float32) + attended).astype(jnp.bfloat16)
    half_width = stream.shape[1]
    myself = lax.axis_index("heads")
    owner_count = lax.axis_size("rows")
    block_count = active.shape[1]
    request_count = active.shape[0]
    by_block = jnp.transpose(active)
    earlier = jnp.cumsum(by_block, axis=1) - by_block
    slot_ids = jnp.arange(CAP, dtype=jnp.int32)[None, :, None]
    slot_table = by_block[:, None, :] * (earlier[:, None, :] == slot_ids).astype(jnp.int32)
    selector3 = jnp.repeat(slot_table, owner_count // block_count, axis=0)
    selector = selector3.reshape(owner_count * CAP, request_count)
    outgoing = jnp.einsum(
        "ocr,rd->ocd",
        selector3.astype(jnp.bfloat16),
        stream,
        preferred_element_type=jnp.float32,
    ).astype(jnp.bfloat16)
    incoming_half = lax.all_to_all(outgoing, "rows", split_axis=0, concat_axis=0, tiled=True)
    incoming = normalize_rows(join_halves(incoming_half.reshape(owner_count * CAP, -1), myself), norm_gain)
    kept, given = swiglu_halves(
        incoming, cold_gate, cold_up, cold_down, myself, (owner_count, CAP)
    )
    given_narrow = partner(given.astype(jnp.bfloat16), "heads", 0)
    owner_sum = (kept + given_narrow.astype(jnp.float32)).astype(jnp.bfloat16)
    stream_late, owner_sum = lax.optimization_barrier((stream, owner_sum))
    returned = lax.all_to_all(owner_sum, "rows", split_axis=0, concat_axis=0, tiled=True)
    normed = normalize_rows(join_halves(stream_late, myself), norm_gain)
    hot_kept, hot_given = swiglu_halves(
        normed, hot_gate, hot_up, hot_down, myself, (request_count,)
    )
    hot_total = hot_kept + partner(hot_given, "heads", 0)
    cold_sum = collect_rows(
        selector.astype(jnp.float32),
        returned.reshape(owner_count * CAP, -1).astype(jnp.float32),
    )
    result = stream.astype(jnp.float32) + hot_total + cold_sum
    return result.astype(jnp.bfloat16)


def solution(mesh):
    return jax.shard_map(
        local,
        mesh=mesh,
        in_specs=(
            P(("groups", "rows"), "heads"),
            P(("groups", "rows"), "heads"),
            P(("groups", "rows"), "heads", None, None),
            P(("groups", "rows"), "heads", None, None),
            P(("groups", "rows"), "heads", None),
            P(("groups", "rows"), "heads", None),
            P(("groups", "rows")),
            P(),
            P("heads", None),
            P("heads", None),
            P("heads", None),
            P(("rows", "heads"), None),
            P(("rows", "heads"), None),
            P(("rows", "heads"), None),
            P(("groups", "rows"), None),
        ),
        out_specs=P(("groups", "rows"), "heads"),
        check_vma=False,
    )
```

```python
import jax
import jax.numpy as jnp
from jax import lax
from jax.sharding import PartitionSpec as P

HD = 128
D = 8192
CAP = 2


def partner(block, axis, bit):
    count = lax.axis_size(axis)
    route = []
    for low in range(count):
        high = low | 1 << bit
        if high != low and high < count:
            route += [(low, high), (high, low)]
    return lax.ppermute(block, axis, route)


def join_halves(half, myself):
    other = partner(half, "heads", 0)
    low_first = jnp.concatenate([half, other], axis=1)
    high_first = jnp.concatenate([other, half], axis=1)
    return jnp.where(myself == 0, low_first, high_first)


def attention_rows(query, key_cache, value_cache, key_new, value_new, lengths):
    count = key_cache.shape[0]
    kv_local = key_cache.shape[1]
    slots = key_cache.shape[2]
    scale_factor = 1.0 / HD**0.5
    queries = query.reshape(count, kv_local, -1, HD)
    keys_all = jnp.concatenate([key_cache, key_new[:, :, None, :]], axis=2)
    values_all = jnp.concatenate([value_cache, value_new[:, :, None, :]], axis=2)
    scores = (
        jnp.einsum("rgjd,rgpd->rgjp", queries, keys_all, preferred_element_type=jnp.float32)
        * scale_factor
    )
    positions = jnp.arange(slots + 1, dtype=jnp.int32)[None, :]
    visible = ((positions < lengths[:, None]) | (positions == slots))[:, None, None, :]
    scores = lax.optimization_barrier(jnp.where(visible, scores, -1e30))
    highest = jnp.max(scores, axis=-1)
    expons = jnp.where(visible, jnp.exp(scores - highest[..., None]), 0.0)
    totals = jnp.sum(expons, axis=-1)
    weights = (expons / totals[..., None]).astype(jnp.bfloat16)
    blended = jnp.einsum(
        "rgjp,rgpd->rgjd", weights, values_all, preferred_element_type=jnp.float32
    )
    return blended.reshape(count, -1)


def swiglu_rows(normed, gate_rows, up_rows, down_rows):
    gate = jnp.einsum("rd,nd->rn", normed, gate_rows, preferred_element_type=jnp.float32)
    upper = jnp.einsum("rd,nd->rn", normed, up_rows, preferred_element_type=jnp.float32)
    hidden = (jax.nn.silu(gate) * upper).astype(jnp.bfloat16)
    return jnp.dot(hidden, down_rows, preferred_element_type=jnp.float32)


def swiglu_halves(normed, gate_rows, up_rows, down_rows, myself, rows_shape):
    gate = jnp.einsum("rd,nd->rn", normed, gate_rows, preferred_element_type=jnp.float32)
    upper = jnp.einsum("rd,nd->rn", normed, up_rows, preferred_element_type=jnp.float32)
    hidden = (jax.nn.silu(gate) * upper).astype(jnp.bfloat16)
    hidden = hidden.reshape(rows_shape + hidden.shape[-1:])
    half_width = down_rows.shape[1] // 2
    down_given = lax.dynamic_slice_in_dim(down_rows, (1 - myself) * half_width, half_width, 1)
    down_kept = lax.dynamic_slice_in_dim(down_rows, myself * half_width, half_width, 1)
    given = jnp.einsum("...n,nd->...d", hidden, down_given, preferred_element_type=jnp.float32)
    kept = jnp.einsum("...n,nd->...d", hidden, down_kept, preferred_element_type=jnp.float32)
    return kept, given


def collect_rows(selector, returned):
    return lax.dot_general(
        selector,
        returned,
        (((0,), (0,)), ((), ())),
        precision=lax.Precision.HIGHEST,
        preferred_element_type=jnp.float32,
    )


def local(
    residual_in,
    query,
    key_cache,
    value_cache,
    key_new,
    value_new,
    lengths,
    norm_gain,
    hot_gate,
    hot_up,
    hot_down,
    cold_gate,
    cold_up,
    cold_down,
    active,
):
    attended = attention_rows(query, key_cache, value_cache, key_new, value_new, lengths)
    stream = (residual_in.astype(jnp.float32) + attended).astype(jnp.bfloat16)
    half_width = stream.shape[1]
    myself = lax.axis_index("heads")
    local_wide = stream.astype(jnp.float32)
    square_part = jnp.sum(local_wide * local_wide, axis=-1)
    square_total = square_part + partner(square_part, "heads", 0)
    gain_half = lax.dynamic_slice_in_dim(norm_gain, myself * half_width, half_width)
    scaled = (
        local_wide * lax.rsqrt(square_total / D + 1e-05)[:, None] * gain_half.astype(jnp.float32)
    )
    normed = join_halves(scaled.astype(jnp.bfloat16), myself)
    owner_count = lax.axis_size("rows")
    block_count = active.shape[1]
    request_count = active.shape[0]
    by_block = jnp.transpose(active)
    earlier = jnp.cumsum(by_block, axis=1) - by_block
    slot_ids = jnp.arange(CAP, dtype=jnp.int32)[None, :, None]
    slot_table = by_block[:, None, :] * (earlier[:, None, :] == slot_ids).astype(jnp.int32)
    selector3 = jnp.repeat(slot_table, owner_count // block_count, axis=0)
    selector = selector3.reshape(owner_count * CAP, request_count)
    outgoing = jnp.einsum(
        "ocr,rd->ocd",
        selector3.astype(jnp.bfloat16),
        scaled.astype(jnp.bfloat16),
        preferred_element_type=jnp.float32,
    ).astype(jnp.bfloat16)
    incoming_half = lax.all_to_all(outgoing, "rows", split_axis=0, concat_axis=0, tiled=True)
    incoming = join_halves(incoming_half.reshape(owner_count * CAP, -1), myself)
    kept, given = swiglu_halves(
        incoming, cold_gate, cold_up, cold_down, myself, (owner_count, CAP)
    )
    given_narrow = partner(given.astype(jnp.bfloat16), "heads", 0)
    owner_sum = (kept + given_narrow.astype(jnp.float32)).astype(jnp.bfloat16)
    normed_late, owner_sum = lax.optimization_barrier((normed, owner_sum))
    returned = lax.all_to_all(owner_sum, "rows", split_axis=0, concat_axis=0, tiled=True)
    hot_kept, hot_given = swiglu_halves(
        normed_late, hot_gate, hot_up, hot_down, myself, (request_count,)
    )
    hot_total = hot_kept + partner(hot_given, "heads", 0)
    cold_sum = collect_rows(
        selector.astype(jnp.float32),
        returned.reshape(owner_count * CAP, -1).astype(jnp.float32),
    )
    result = stream.astype(jnp.float32) + hot_total + cold_sum
    return result.astype(jnp.bfloat16)


def solution(mesh):
    return jax.shard_map(
        local,
        mesh=mesh,
        in_specs=(
            P(("groups", "rows"), "heads"),
            P(("groups", "rows"), "heads"),
            P(("groups", "rows"), "heads", None, None),
            P(("groups", "rows"), "heads", None, None),
            P(("groups", "rows"), "heads", None),
            P(("groups", "rows"), "heads", None),
            P(("groups", "rows")),
            P(),
            P("heads", None),
            P("heads", None),
            P("heads", None),
            P(("rows", "heads"), None),
            P(("rows", "heads"), None),
            P(("rows", "heads"), None),
            P(("groups", "rows"), None),
        ),
        out_specs=P(("groups", "rows"), "heads"),
        check_vma=False,
    )
```

```python
import jax
import jax.numpy as jnp
from jax import lax
from jax.sharding import PartitionSpec as P

HD = 128
D = 8192
CAP = 2


def partner(block, axis, bit):
    count = lax.axis_size(axis)
    route = []
    for low in range(count):
        high = low | 1 << bit
        if high != low and high < count:
            route += [(low, high), (high, low)]
    return lax.ppermute(block, axis, route)


def join_halves(half, myself):
    other = partner(half, "heads", 0)
    low_first = jnp.concatenate([half, other], axis=1)
    high_first = jnp.concatenate([other, half], axis=1)
    return jnp.where(myself == 0, low_first, high_first)


def attention_rows(query, key_cache, value_cache, key_new, value_new, lengths):
    count = key_cache.shape[0]
    kv_local = key_cache.shape[1]
    slots = key_cache.shape[2]
    scale_factor = 1.0 / HD**0.5
    queries = query.reshape(count, kv_local, -1, HD)
    copies = (count, kv_local, 8, HD)
    keys_all = jnp.concatenate(
        [key_cache, jnp.broadcast_to(key_new[:, :, None, :], copies)], axis=2
    )
    values_all = jnp.concatenate(
        [value_cache, jnp.broadcast_to(value_new[:, :, None, :], copies)], axis=2
    )
    scores = (
        jnp.einsum("rgjd,rgpd->rgjp", queries, keys_all, preferred_element_type=jnp.float32)
        * scale_factor
    )
    positions = jnp.arange(slots + 8, dtype=jnp.int32)[None, :]
    visible = ((positions < lengths[:, None]) | (positions == slots))[:, None, None, :]
    scores = jnp.where(visible, scores, -1e30)
    highest = jnp.max(scores, axis=-1)
    expons = jnp.where(visible, jnp.exp(scores - highest[..., None]), 0.0)
    totals = jnp.sum(expons, axis=-1)
    weights = (expons / totals[..., None]).astype(jnp.bfloat16)
    blended = jnp.einsum(
        "rgjp,rgpd->rgjd", weights, values_all, preferred_element_type=jnp.float32
    )
    return blended.reshape(count, -1)


def swiglu_rows(normed, gate_rows, up_rows, down_rows):
    gate = jnp.einsum("rd,nd->rn", normed, gate_rows, preferred_element_type=jnp.float32)
    upper = jnp.einsum("rd,nd->rn", normed, up_rows, preferred_element_type=jnp.float32)
    hidden = (jax.nn.silu(gate) * upper).astype(jnp.bfloat16)
    return jnp.dot(hidden, down_rows, preferred_element_type=jnp.float32)


def swiglu_halves(normed, gate_rows, up_rows, down_rows, myself, rows_shape):
    gate = jnp.einsum("rd,nd->rn", normed, gate_rows, preferred_element_type=jnp.float32)
    upper = jnp.einsum("rd,nd->rn", normed, up_rows, preferred_element_type=jnp.float32)
    hidden = (jax.nn.silu(gate) * upper).astype(jnp.bfloat16)
    hidden = hidden.reshape(rows_shape + hidden.shape[-1:])
    half_width = down_rows.shape[1] // 2
    down_given = lax.dynamic_slice_in_dim(down_rows, (1 - myself) * half_width, half_width, 1)
    down_kept = lax.dynamic_slice_in_dim(down_rows, myself * half_width, half_width, 1)
    given = jnp.einsum("...n,nd->...d", hidden, down_given, preferred_element_type=jnp.float32)
    kept = jnp.einsum("...n,nd->...d", hidden, down_kept, preferred_element_type=jnp.float32)
    return kept, given


def collect_rows(selector, returned):
    return lax.dot_general(
        selector,
        returned,
        (((0,), (0,)), ((), ())),
        precision=lax.Precision.HIGHEST,
        preferred_element_type=jnp.float32,
    )


def local(
    residual_in,
    query,
    key_cache,
    value_cache,
    key_new,
    value_new,
    lengths,
    norm_gain,
    hot_gate,
    hot_up,
    hot_down,
    cold_gate,
    cold_up,
    cold_down,
    active,
):
    attended = attention_rows(query, key_cache, value_cache, key_new, value_new, lengths)
    stream = (residual_in.astype(jnp.float32) + attended).astype(jnp.bfloat16)
    half_width = stream.shape[1]
    myself = lax.axis_index("heads")
    local_wide = stream.astype(jnp.float32)
    square_part = jnp.sum(local_wide * local_wide, axis=-1)
    square_total = square_part + partner(square_part, "heads", 0)
    gain_half = lax.dynamic_slice_in_dim(norm_gain, myself * half_width, half_width)
    scaled = (
        local_wide * lax.rsqrt(square_total / D + 1e-05)[:, None] * gain_half.astype(jnp.float32)
    )
    normed = join_halves(scaled.astype(jnp.bfloat16), myself)
    owner_count = lax.axis_size("rows")
    block_count = active.shape[1]
    request_count = active.shape[0]
    by_block = jnp.transpose(active)
    earlier = jnp.cumsum(by_block, axis=1) - by_block
    slot_ids = jnp.arange(CAP, dtype=jnp.int32)[None, :, None]
    slot_table = by_block[:, None, :] * (earlier[:, None, :] == slot_ids).astype(jnp.int32)
    selector3 = jnp.repeat(slot_table, owner_count // block_count, axis=0)
    selector = selector3.reshape(owner_count * CAP, request_count)
    outgoing = jnp.einsum(
        "ocr,rd->ocd",
        selector3.astype(jnp.bfloat16),
        scaled.astype(jnp.bfloat16),
        preferred_element_type=jnp.float32,
    ).astype(jnp.bfloat16)
    incoming_half = lax.all_to_all(outgoing, "rows", split_axis=0, concat_axis=0, tiled=True)
    incoming = join_halves(incoming_half.reshape(owner_count * CAP, -1), myself)
    kept, given = swiglu_halves(
        incoming, cold_gate, cold_up, cold_down, myself, (owner_count, CAP)
    )
    given_narrow = partner(given.astype(jnp.bfloat16), "heads", 0)
    owner_sum = (kept + given_narrow.astype(jnp.float32)).astype(jnp.bfloat16)
    normed_late, owner_sum = lax.optimization_barrier((normed, owner_sum))
    returned = lax.all_to_all(owner_sum, "rows", split_axis=0, concat_axis=0, tiled=True)
    hot_kept, hot_given = swiglu_halves(
        normed_late, hot_gate, hot_up, hot_down, myself, (request_count,)
    )
    hot_total = hot_kept + partner(hot_given, "heads", 0)
    cold_sum = collect_rows(
        selector.astype(jnp.float32),
        returned.reshape(owner_count * CAP, -1).astype(jnp.float32),
    )
    result = stream.astype(jnp.float32) + hot_total + cold_sum
    return result.astype(jnp.bfloat16)


def solution(mesh):
    return jax.shard_map(
        local,
        mesh=mesh,
        in_specs=(
            P(("groups", "rows"), "heads"),
            P(("groups", "rows"), "heads"),
            P(("groups", "rows"), "heads", None, None),
            P(("groups", "rows"), "heads", None, None),
            P(("groups", "rows"), "heads", None),
            P(("groups", "rows"), "heads", None),
            P(("groups", "rows")),
            P(),
            P("heads", None),
            P("heads", None),
            P("heads", None),
            P(("rows", "heads"), None),
            P(("rows", "heads"), None),
            P(("rows", "heads"), None),
            P(("groups", "rows"), None),
        ),
        out_specs=P(("groups", "rows"), "heads"),
        check_vma=False,
    )
```

```python
import jax
import jax.numpy as jnp
from jax import lax
from jax.sharding import PartitionSpec as P

HD = 128
D = 8192
CAP = 2


def partner(block, axis, bit):
    count = lax.axis_size(axis)
    route = []
    for low in range(count):
        high = low | 1 << bit
        if high != low and high < count:
            route += [(low, high), (high, low)]
    return lax.ppermute(block, axis, route)


def join_halves(half, myself):
    other = partner(half, "heads", 0)
    low_first = jnp.concatenate([half, other], axis=1)
    high_first = jnp.concatenate([other, half], axis=1)
    return jnp.where(myself == 0, low_first, high_first)


def attention_rows(query, key_cache, value_cache, key_new, value_new, lengths):
    count = key_cache.shape[0]
    kv_local = key_cache.shape[1]
    slots = key_cache.shape[2]
    scale_factor = 1.0 / HD**0.5
    queries = query.reshape(count, kv_local, -1, HD)
    copies = (count, kv_local, 8, HD)
    keys_all = jnp.concatenate(
        [key_cache, jnp.broadcast_to(key_new[:, :, None, :], copies)], axis=2
    )
    values_all = jnp.concatenate(
        [value_cache, jnp.broadcast_to(value_new[:, :, None, :], copies)], axis=2
    )
    scores = lax.optimization_barrier(
        jnp.einsum("rgjd,rgpd->rgjp", queries, keys_all, preferred_element_type=jnp.float32)
        * scale_factor
    )
    positions = jnp.arange(slots + 8, dtype=jnp.int32)[None, :]
    visible = ((positions < lengths[:, None]) | (positions == slots))[:, None, None, :]
    scores = jnp.where(visible, scores, -1e30)
    highest = jnp.max(scores, axis=-1)
    expons = jnp.where(visible, jnp.exp(scores - highest[..., None]), 0.0)
    totals = jnp.sum(expons, axis=-1)
    weights = (expons / totals[..., None]).astype(jnp.bfloat16)
    blended = jnp.einsum(
        "rgjp,rgpd->rgjd", weights, values_all, preferred_element_type=jnp.float32
    )
    return blended.reshape(count, -1)


def swiglu_rows(normed, gate_rows, up_rows, down_rows):
    gate = jnp.einsum("rd,nd->rn", normed, gate_rows, preferred_element_type=jnp.float32)
    upper = jnp.einsum("rd,nd->rn", normed, up_rows, preferred_element_type=jnp.float32)
    hidden = (jax.nn.silu(gate) * upper).astype(jnp.bfloat16)
    return jnp.dot(hidden, down_rows, preferred_element_type=jnp.float32)


def swiglu_halves(normed, gate_rows, up_rows, down_rows, myself, rows_shape):
    gate = jnp.einsum("rd,nd->rn", normed, gate_rows, preferred_element_type=jnp.float32)
    upper = jnp.einsum("rd,nd->rn", normed, up_rows, preferred_element_type=jnp.float32)
    hidden = (jax.nn.silu(gate) * upper).astype(jnp.bfloat16)
    hidden = hidden.reshape(rows_shape + hidden.shape[-1:])
    half_width = down_rows.shape[1] // 2
    down_given = lax.dynamic_slice_in_dim(down_rows, (1 - myself) * half_width, half_width, 1)
    down_kept = lax.dynamic_slice_in_dim(down_rows, myself * half_width, half_width, 1)
    given = jnp.einsum("...n,nd->...d", hidden, down_given, preferred_element_type=jnp.float32)
    kept = jnp.einsum("...n,nd->...d", hidden, down_kept, preferred_element_type=jnp.float32)
    return kept, given


def collect_rows(selector, returned):
    return lax.dot_general(
        selector,
        returned,
        (((0,), (0,)), ((), ())),
        precision=lax.Precision.HIGHEST,
        preferred_element_type=jnp.float32,
    )


def local(
    residual_in,
    query,
    key_cache,
    value_cache,
    key_new,
    value_new,
    lengths,
    norm_gain,
    hot_gate,
    hot_up,
    hot_down,
    cold_gate,
    cold_up,
    cold_down,
    active,
):
    attended = attention_rows(query, key_cache, value_cache, key_new, value_new, lengths)
    stream = (residual_in.astype(jnp.float32) + attended).astype(jnp.bfloat16)
    half_width = stream.shape[1]
    myself = lax.axis_index("heads")
    local_wide = stream.astype(jnp.float32)
    square_part = jnp.sum(local_wide * local_wide, axis=-1)
    square_total = square_part + partner(square_part, "heads", 0)
    gain_half = lax.dynamic_slice_in_dim(norm_gain, myself * half_width, half_width)
    scaled = (
        local_wide * lax.rsqrt(square_total / D + 1e-05)[:, None] * gain_half.astype(jnp.float32)
    )
    normed = join_halves(scaled.astype(jnp.bfloat16), myself)
    owner_count = lax.axis_size("rows")
    block_count = active.shape[1]
    request_count = active.shape[0]
    by_block = jnp.transpose(active)
    earlier = jnp.cumsum(by_block, axis=1) - by_block
    slot_ids = jnp.arange(CAP, dtype=jnp.int32)[None, :, None]
    slot_table = by_block[:, None, :] * (earlier[:, None, :] == slot_ids).astype(jnp.int32)
    selector3 = jnp.repeat(slot_table, owner_count // block_count, axis=0)
    selector = selector3.reshape(owner_count * CAP, request_count)
    outgoing = jnp.einsum(
        "ocr,rd->ocd",
        selector3.astype(jnp.bfloat16),
        scaled.astype(jnp.bfloat16),
        preferred_element_type=jnp.float32,
    ).astype(jnp.bfloat16)
    incoming_half = lax.all_to_all(outgoing, "rows", split_axis=0, concat_axis=0, tiled=True)
    incoming = join_halves(incoming_half.reshape(owner_count * CAP, -1), myself)
    kept, given = swiglu_halves(
        incoming, cold_gate, cold_up, cold_down, myself, (owner_count, CAP)
    )
    given_narrow = partner(given.astype(jnp.bfloat16), "heads", 0)
    owner_sum = (kept + given_narrow.astype(jnp.float32)).astype(jnp.bfloat16)
    normed_late, owner_sum = lax.optimization_barrier((normed, owner_sum))
    returned = lax.all_to_all(owner_sum, "rows", split_axis=0, concat_axis=0, tiled=True)
    hot_kept, hot_given = swiglu_halves(
        normed_late, hot_gate, hot_up, hot_down, myself, (request_count,)
    )
    hot_total = hot_kept + partner(hot_given, "heads", 0)
    cold_sum = collect_rows(
        selector.astype(jnp.float32),
        returned.reshape(owner_count * CAP, -1).astype(jnp.float32),
    )
    result = stream.astype(jnp.float32) + hot_total + cold_sum
    return result.astype(jnp.bfloat16)


def solution(mesh):
    return jax.shard_map(
        local,
        mesh=mesh,
        in_specs=(
            P(("groups", "rows"), "heads"),
            P(("groups", "rows"), "heads"),
            P(("groups", "rows"), "heads", None, None),
            P(("groups", "rows"), "heads", None, None),
            P(("groups", "rows"), "heads", None),
            P(("groups", "rows"), "heads", None),
            P(("groups", "rows")),
            P(),
            P("heads", None),
            P("heads", None),
            P("heads", None),
            P(("rows", "heads"), None),
            P(("rows", "heads"), None),
            P(("rows", "heads"), None),
            P(("groups", "rows"), None),
        ),
        out_specs=P(("groups", "rows"), "heads"),
        check_vma=False,
    )
```

```python
import jax
import jax.numpy as jnp
from jax import lax
from jax.sharding import PartitionSpec as P

HD = 128
D = 8192
CAP = 2


def partner(block, axis, bit):
    count = lax.axis_size(axis)
    route = []
    for low in range(count):
        high = low | 1 << bit
        if high != low and high < count:
            route += [(low, high), (high, low)]
    return lax.ppermute(block, axis, route)


def join_halves(half, myself):
    other = partner(half, "heads", 0)
    low_first = jnp.concatenate([half, other], axis=1)
    high_first = jnp.concatenate([other, half], axis=1)
    return jnp.where(myself == 0, low_first, high_first)


def attention_rows(query, key_cache, value_cache, key_new, value_new, lengths):
    count = key_cache.shape[0]
    kv_local = key_cache.shape[1]
    slots = key_cache.shape[2]
    scale_factor = 1.0 / HD**0.5
    queries = query.reshape(count, kv_local, -1, HD)
    news = jnp.stack([key_new, value_new])
    news = lax.optimization_barrier(
        jnp.broadcast_to(news[:, :, :, None, :], (2, count, kv_local, 8, HD))
    )
    keys_all = jnp.concatenate([key_cache, news[0]], axis=2)
    values_all = jnp.concatenate([value_cache, news[1]], axis=2)
    scores = lax.optimization_barrier(
        jnp.einsum("rgjd,rgpd->rgjp", queries, keys_all, preferred_element_type=jnp.float32)
        * scale_factor
    )
    positions = jnp.arange(slots + 8, dtype=jnp.int32)[None, :]
    visible = ((positions < lengths[:, None]) | (positions == slots))[:, None, None, :]
    scores = jnp.where(visible, scores, -1e30)
    highest = jnp.max(scores, axis=-1)
    expons = jnp.where(visible, jnp.exp(scores - highest[..., None]), 0.0)
    totals = jnp.sum(expons, axis=-1)
    weights = (expons / totals[..., None]).astype(jnp.bfloat16)
    blended = jnp.einsum(
        "rgjp,rgpd->rgjd", weights, values_all, preferred_element_type=jnp.float32
    )
    return blended.reshape(count, -1)


def swiglu_rows(normed, gate_rows, up_rows, down_rows):
    gate = jnp.einsum("rd,nd->rn", normed, gate_rows, preferred_element_type=jnp.float32)
    upper = jnp.einsum("rd,nd->rn", normed, up_rows, preferred_element_type=jnp.float32)
    hidden = (jax.nn.silu(gate) * upper).astype(jnp.bfloat16)
    return jnp.dot(hidden, down_rows, preferred_element_type=jnp.float32)


def swiglu_halves(normed, gate_rows, up_rows, down_rows, myself, rows_shape):
    gate = jnp.einsum("rd,nd->rn", normed, gate_rows, preferred_element_type=jnp.float32)
    upper = jnp.einsum("rd,nd->rn", normed, up_rows, preferred_element_type=jnp.float32)
    hidden = (jax.nn.silu(gate) * upper).astype(jnp.bfloat16)
    hidden = hidden.reshape(rows_shape + hidden.shape[-1:])
    half_width = down_rows.shape[1] // 2
    down_given = lax.dynamic_slice_in_dim(down_rows, (1 - myself) * half_width, half_width, 1)
    down_kept = lax.dynamic_slice_in_dim(down_rows, myself * half_width, half_width, 1)
    given = jnp.einsum("...n,nd->...d", hidden, down_given, preferred_element_type=jnp.float32)
    kept = jnp.einsum("...n,nd->...d", hidden, down_kept, preferred_element_type=jnp.float32)
    return kept, given


def collect_rows(selector, returned):
    return lax.dot_general(
        selector,
        returned,
        (((0,), (0,)), ((), ())),
        precision=lax.Precision.HIGHEST,
        preferred_element_type=jnp.float32,
    )


def local(
    residual_in,
    query,
    key_cache,
    value_cache,
    key_new,
    value_new,
    lengths,
    norm_gain,
    hot_gate,
    hot_up,
    hot_down,
    cold_gate,
    cold_up,
    cold_down,
    active,
):
    attended = attention_rows(query, key_cache, value_cache, key_new, value_new, lengths)
    stream = (residual_in.astype(jnp.float32) + attended).astype(jnp.bfloat16)
    half_width = stream.shape[1]
    myself = lax.axis_index("heads")
    local_wide = stream.astype(jnp.float32)
    square_part = jnp.sum(local_wide * local_wide, axis=-1)
    square_total = square_part + partner(square_part, "heads", 0)
    gain_half = lax.dynamic_slice_in_dim(norm_gain, myself * half_width, half_width)
    scaled = (
        local_wide * lax.rsqrt(square_total / D + 1e-05)[:, None] * gain_half.astype(jnp.float32)
    )
    normed = join_halves(scaled.astype(jnp.bfloat16), myself)
    owner_count = lax.axis_size("rows")
    block_count = active.shape[1]
    request_count = active.shape[0]
    by_block = jnp.transpose(active)
    earlier = jnp.cumsum(by_block, axis=1) - by_block
    slot_ids = jnp.arange(CAP, dtype=jnp.int32)[None, :, None]
    slot_table = by_block[:, None, :] * (earlier[:, None, :] == slot_ids).astype(jnp.int32)
    selector3 = jnp.repeat(slot_table, owner_count // block_count, axis=0)
    selector = selector3.reshape(owner_count * CAP, request_count)
    outgoing = jnp.einsum(
        "ocr,rd->ocd",
        selector3.astype(jnp.bfloat16),
        scaled.astype(jnp.bfloat16),
        preferred_element_type=jnp.float32,
    ).astype(jnp.bfloat16)
    incoming_half = lax.all_to_all(outgoing, "rows", split_axis=0, concat_axis=0, tiled=True)
    incoming = join_halves(incoming_half.reshape(owner_count * CAP, -1), myself)
    kept, given = swiglu_halves(
        incoming, cold_gate, cold_up, cold_down, myself, (owner_count, CAP)
    )
    given_narrow = partner(given.astype(jnp.bfloat16), "heads", 0)
    owner_sum = (kept + given_narrow.astype(jnp.float32)).astype(jnp.bfloat16)
    normed_late, owner_sum = lax.optimization_barrier((normed, owner_sum))
    returned = lax.all_to_all(owner_sum, "rows", split_axis=0, concat_axis=0, tiled=True)
    hot_kept, hot_given = swiglu_halves(
        normed_late, hot_gate, hot_up, hot_down, myself, (request_count,)
    )
    hot_total = hot_kept + partner(hot_given, "heads", 0)
    cold_sum = collect_rows(
        selector.astype(jnp.float32),
        returned.reshape(owner_count * CAP, -1).astype(jnp.float32),
    )
    result = stream.astype(jnp.float32) + hot_total + cold_sum
    return result.astype(jnp.bfloat16)


def solution(mesh):
    return jax.shard_map(
        local,
        mesh=mesh,
        in_specs=(
            P(("groups", "rows"), "heads"),
            P(("groups", "rows"), "heads"),
            P(("groups", "rows"), "heads", None, None),
            P(("groups", "rows"), "heads", None, None),
            P(("groups", "rows"), "heads", None),
            P(("groups", "rows"), "heads", None),
            P(("groups", "rows")),
            P(),
            P("heads", None),
            P("heads", None),
            P("heads", None),
            P(("rows", "heads"), None),
            P(("rows", "heads"), None),
            P(("rows", "heads"), None),
            P(("groups", "rows"), None),
        ),
        out_specs=P(("groups", "rows"), "heads"),
        check_vma=False,
    )
```

```python
import jax
import jax.numpy as jnp
from jax import lax
from jax.sharding import PartitionSpec as P

HD = 128
D = 8192
CAP = 2


def partner(block, axis, bit):
    count = lax.axis_size(axis)
    route = []
    for low in range(count):
        high = low | 1 << bit
        if high != low and high < count:
            route += [(low, high), (high, low)]
    return lax.ppermute(block, axis, route)


def join_halves(half, myself):
    other = partner(half, "heads", 0)
    low_first = jnp.concatenate([half, other], axis=1)
    high_first = jnp.concatenate([other, half], axis=1)
    return jnp.where(myself == 0, low_first, high_first)


def attention_rows(query, key_cache, value_cache, key_new, value_new, lengths):
    count = key_cache.shape[0]
    kv_local = key_cache.shape[1]
    slots = key_cache.shape[2]
    scale_factor = 1.0 / HD**0.5
    queries = query.reshape(count, kv_local, -1, HD)
    keys_all = jnp.concatenate([key_cache, key_new[:, :, None, :]], axis=2)
    values_all = jnp.concatenate([value_cache, value_new[:, :, None, :]], axis=2)
    scores = (
        jnp.einsum("rgjd,rgpd->rgjp", queries, keys_all, preferred_element_type=jnp.float32)
        * scale_factor
    )
    positions = jnp.arange(slots + 1, dtype=jnp.int32)[None, :]
    visible = ((positions < lengths[:, None]) | (positions == slots))[:, None, None, :]
    scores = jnp.where(visible, scores, -1e30)
    highest = jnp.max(scores, axis=-1)
    expons = jnp.where(visible, jnp.exp(scores - highest[..., None]), 0.0)
    totals = jnp.sum(expons, axis=-1)
    weights = (expons / totals[..., None]).astype(jnp.bfloat16)
    blended = jnp.einsum(
        "rgjp,rgpd->rgjd", weights, values_all, preferred_element_type=jnp.float32
    )
    return blended.reshape(count, -1)


def swiglu_rows(normed, gate_rows, up_rows, down_rows):
    gate = jnp.einsum("rd,nd->rn", normed, gate_rows, preferred_element_type=jnp.float32)
    upper = jnp.einsum("rd,nd->rn", normed, up_rows, preferred_element_type=jnp.float32)
    hidden = (jax.nn.silu(gate) * upper).astype(jnp.bfloat16)
    return jnp.dot(hidden, down_rows, preferred_element_type=jnp.float32)


def swiglu_halves(normed, gate_rows, up_rows, down_rows, myself, rows_shape):
    gate = jnp.einsum("rd,nd->rn", normed, gate_rows, preferred_element_type=jnp.float32)
    upper = jnp.einsum("rd,nd->rn", normed, up_rows, preferred_element_type=jnp.float32)
    hidden = (jax.nn.silu(gate) * upper).astype(jnp.bfloat16)
    hidden = hidden.reshape(rows_shape + hidden.shape[-1:])
    half_width = down_rows.shape[1] // 2
    down_given = lax.dynamic_slice_in_dim(down_rows, (1 - myself) * half_width, half_width, 1)
    down_kept = lax.dynamic_slice_in_dim(down_rows, myself * half_width, half_width, 1)
    given = jnp.einsum("...n,nd->...d", hidden, down_given, preferred_element_type=jnp.float32)
    kept = jnp.einsum("...n,nd->...d", hidden, down_kept, preferred_element_type=jnp.float32)
    return kept, given


def collect_rows(selector, returned):
    return lax.dot_general(
        selector,
        returned,
        (((0,), (0,)), ((), ())),
        precision=lax.Precision.HIGHEST,
        preferred_element_type=jnp.float32,
    )


def local(
    residual_in,
    query,
    key_cache,
    value_cache,
    key_new,
    value_new,
    lengths,
    norm_gain,
    hot_gate,
    hot_up,
    hot_down,
    cold_gate,
    cold_up,
    cold_down,
    active,
):
    attended = attention_rows(query, key_cache, value_cache, key_new, value_new, lengths)
    stream = (residual_in.astype(jnp.float32) + attended).astype(jnp.bfloat16)
    half_width = stream.shape[1]
    myself = lax.axis_index("heads")
    local_wide = stream.astype(jnp.float32)
    square_part = jnp.sum(local_wide * local_wide, axis=-1)
    square_total = square_part + partner(square_part, "heads", 0)
    gain_half = lax.dynamic_slice_in_dim(norm_gain, myself * half_width, half_width)
    scaled = (
        local_wide * lax.rsqrt(square_total / D + 1e-05)[:, None] * gain_half.astype(jnp.float32)
    )
    normed = join_halves(scaled.astype(jnp.bfloat16), myself)
    owner_count = lax.axis_size("rows")
    block_count = active.shape[1]
    request_count = active.shape[0]
    by_block = jnp.transpose(active)
    earlier = jnp.cumsum(by_block, axis=1) - by_block
    slot_ids = jnp.arange(CAP, dtype=jnp.int32)[None, :, None]
    slot_table = by_block[:, None, :] * (earlier[:, None, :] == slot_ids).astype(jnp.int32)
    selector3 = jnp.repeat(slot_table, owner_count // block_count, axis=0)
    selector = selector3.reshape(owner_count * CAP, request_count)
    outgoing = jnp.einsum(
        "ocr,rd->ocd",
        selector3.astype(jnp.bfloat16),
        scaled.astype(jnp.bfloat16),
        preferred_element_type=jnp.float32,
    ).astype(jnp.bfloat16)
    incoming_half = lax.all_to_all(outgoing, "rows", split_axis=0, concat_axis=0, tiled=True)
    incoming = join_halves(incoming_half.reshape(owner_count * CAP, -1), myself)
    kept, given = swiglu_halves(
        incoming, cold_gate, cold_up, cold_down, myself, (owner_count, CAP)
    )
    given_narrow = partner(given.astype(jnp.bfloat16), "heads", 0)
    owner_sum = (kept + given_narrow.astype(jnp.float32)).astype(jnp.bfloat16)
    normed_late, owner_sum = lax.optimization_barrier((normed, owner_sum))
    returned = lax.all_to_all(owner_sum, "rows", split_axis=0, concat_axis=0, tiled=True)
    hot_kept, hot_given = swiglu_halves(
        normed_late, hot_gate, hot_up, hot_down, myself, (request_count,)
    )
    hot_received = partner(hot_given, "heads", 0)
    settled = lax.optimization_barrier(stream.astype(jnp.float32) + hot_kept)
    cold_sum = collect_rows(
        selector.astype(jnp.float32),
        returned.reshape(owner_count * CAP, -1).astype(jnp.float32),
    )
    result = settled + hot_received + cold_sum
    return result.astype(jnp.bfloat16)


def solution(mesh):
    return jax.shard_map(
        local,
        mesh=mesh,
        in_specs=(
            P(("groups", "rows"), "heads"),
            P(("groups", "rows"), "heads"),
            P(("groups", "rows"), "heads", None, None),
            P(("groups", "rows"), "heads", None, None),
            P(("groups", "rows"), "heads", None),
            P(("groups", "rows"), "heads", None),
            P(("groups", "rows")),
            P(),
            P("heads", None),
            P("heads", None),
            P("heads", None),
            P(("rows", "heads"), None),
            P(("rows", "heads"), None),
            P(("rows", "heads"), None),
            P(("groups", "rows"), None),
        ),
        out_specs=P(("groups", "rows"), "heads"),
        check_vma=False,
    )
```

```python
import jax
import jax.numpy as jnp
from jax import lax
from jax.sharding import PartitionSpec as P

HD = 128
D = 8192
CAP = 2


def partner(block, axis, bit):
    count = lax.axis_size(axis)
    route = []
    for low in range(count):
        high = low | 1 << bit
        if high != low and high < count:
            route += [(low, high), (high, low)]
    return lax.ppermute(block, axis, route)


def join_halves(half, myself):
    other = partner(half, "heads", 0)
    low_first = jnp.concatenate([half, other], axis=1)
    high_first = jnp.concatenate([other, half], axis=1)
    return jnp.where(myself == 0, low_first, high_first)


def attention_rows(query, key_cache, value_cache, key_new, value_new, lengths):
    count = key_cache.shape[0]
    kv_local = key_cache.shape[1]
    slots = key_cache.shape[2]
    scale_factor = 1.0 / HD**0.5
    queries = query.reshape(count, kv_local, -1, HD)
    keys_all = jnp.concatenate([key_cache, key_new[:, :, None, :]], axis=2)
    values_all = jnp.concatenate([value_cache, value_new[:, :, None, :]], axis=2)
    scores = (
        jnp.einsum("rgjd,rgpd->rgjp", queries, keys_all, preferred_element_type=jnp.float32)
        * scale_factor
    )
    positions = jnp.arange(slots + 1, dtype=jnp.int32)[None, :]
    visible = ((positions < lengths[:, None]) | (positions == slots))[:, None, None, :]
    scores = jnp.where(visible, scores, -1e30)
    highest = jnp.max(scores, axis=-1)
    expons = jnp.where(visible, jnp.exp(scores - highest[..., None]), 0.0)
    totals = jnp.sum(expons, axis=-1)
    weights = (expons / totals[..., None]).astype(jnp.bfloat16)
    blended = jnp.einsum(
        "rgjp,rgpd->rgjd", weights, values_all, preferred_element_type=jnp.float32
    )
    return blended.reshape(count, -1)


def swiglu_rows(normed, gate_rows, up_rows, down_rows):
    gate = jnp.einsum("rd,nd->rn", normed, gate_rows, preferred_element_type=jnp.float32)
    upper = jnp.einsum("rd,nd->rn", normed, up_rows, preferred_element_type=jnp.float32)
    hidden = (jax.nn.silu(gate) * upper).astype(jnp.bfloat16)
    return jnp.dot(hidden, down_rows, preferred_element_type=jnp.float32)


def swiglu_halves(normed, gate_rows, up_rows, down_rows, myself, rows_shape):
    gate = jnp.einsum("rd,nd->rn", normed, gate_rows, preferred_element_type=jnp.float32)
    upper = jnp.einsum("rd,nd->rn", normed, up_rows, preferred_element_type=jnp.float32)
    hidden = (jax.nn.silu(gate) * upper).astype(jnp.bfloat16)
    hidden = hidden.reshape(rows_shape + hidden.shape[-1:])
    half_width = down_rows.shape[1] // 2
    down_given = lax.dynamic_slice_in_dim(down_rows, (1 - myself) * half_width, half_width, 1)
    down_kept = lax.dynamic_slice_in_dim(down_rows, myself * half_width, half_width, 1)
    given = jnp.einsum("...n,nd->...d", hidden, down_given, preferred_element_type=jnp.float32)
    kept = jnp.einsum("...n,nd->...d", hidden, down_kept, preferred_element_type=jnp.float32)
    return kept, given


def collect_rows(selector, returned):
    return lax.dot_general(
        selector,
        returned,
        (((0,), (0,)), ((), ())),
        precision=lax.Precision.HIGHEST,
        preferred_element_type=jnp.float32,
    )


def local(
    residual_in,
    query,
    key_cache,
    value_cache,
    key_new,
    value_new,
    lengths,
    norm_gain,
    hot_gate,
    hot_up,
    hot_down,
    cold_gate,
    cold_up,
    cold_down,
    active,
):
    attended = attention_rows(query, key_cache, value_cache, key_new, value_new, lengths)
    stream = (residual_in.astype(jnp.float32) + attended).astype(jnp.bfloat16)
    half_width = stream.shape[1]
    myself = lax.axis_index("heads")
    local_wide = stream.astype(jnp.float32)
    square_part = jnp.sum(local_wide * local_wide, axis=-1)
    square_total = square_part + partner(square_part, "heads", 0)
    gain_half = lax.dynamic_slice_in_dim(norm_gain, myself * half_width, half_width)
    scaled = (
        local_wide * lax.rsqrt(square_total / D + 1e-05)[:, None] * gain_half.astype(jnp.float32)
    )
    normed = join_halves(scaled.astype(jnp.bfloat16), myself)
    owner_count = lax.axis_size("rows")
    block_count = active.shape[1]
    request_count = active.shape[0]
    by_block = jnp.transpose(active)
    earlier = jnp.cumsum(by_block, axis=1) - by_block
    slot_ids = jnp.arange(CAP, dtype=jnp.int32)[None, :, None]
    slot_table = by_block[:, None, :] * (earlier[:, None, :] == slot_ids).astype(jnp.int32)
    selector3 = jnp.repeat(slot_table, owner_count // block_count, axis=0)
    selector = selector3.reshape(owner_count * CAP, request_count)
    outgoing = jnp.einsum(
        "ocr,rd->ocd",
        selector3.astype(jnp.bfloat16),
        scaled.astype(jnp.bfloat16),
        preferred_element_type=jnp.float32,
    ).astype(jnp.bfloat16)
    incoming_half = lax.all_to_all(outgoing, "rows", split_axis=0, concat_axis=0, tiled=True)
    incoming = join_halves(incoming_half.reshape(owner_count * CAP, -1), myself)
    kept, given = swiglu_halves(
        incoming, cold_gate, cold_up, cold_down, myself, (owner_count, CAP)
    )
    given_narrow = partner(given.astype(jnp.bfloat16), "heads", 0)
    owner_sum = (kept + given_narrow.astype(jnp.float32)).astype(jnp.bfloat16)
    normed_late, owner_sum = lax.optimization_barrier((normed, owner_sum))
    returned = lax.all_to_all(owner_sum, "rows", split_axis=0, concat_axis=0, tiled=True)
    hot_kept, hot_given = swiglu_halves(
        normed_late, hot_gate, hot_up, hot_down, myself, (request_count,)
    )
    hot_received = partner(hot_given, "heads", 0)
    settled = lax.optimization_barrier(stream.astype(jnp.float32) + hot_kept)
    cold_sum = jnp.einsum(
        "sr,sd->rd",
        selector.astype(jnp.bfloat16),
        returned.reshape(owner_count * CAP, -1),
        preferred_element_type=jnp.float32,
    )
    result = settled + hot_received + cold_sum
    return result.astype(jnp.bfloat16)


def solution(mesh):
    return jax.shard_map(
        local,
        mesh=mesh,
        in_specs=(
            P(("groups", "rows"), "heads"),
            P(("groups", "rows"), "heads"),
            P(("groups", "rows"), "heads", None, None),
            P(("groups", "rows"), "heads", None, None),
            P(("groups", "rows"), "heads", None),
            P(("groups", "rows"), "heads", None),
            P(("groups", "rows")),
            P(),
            P("heads", None),
            P("heads", None),
            P("heads", None),
            P(("rows", "heads"), None),
            P(("rows", "heads"), None),
            P(("rows", "heads"), None),
            P(("groups", "rows"), None),
        ),
        out_specs=P(("groups", "rows"), "heads"),
        check_vma=False,
    )
```

```python
import jax
import jax.numpy as jnp
from jax import lax
from jax.sharding import PartitionSpec as P

HD = 128
D = 8192
CAP = 2


def partner(block, axis, bit):
    count = lax.axis_size(axis)
    route = []
    for low in range(count):
        high = low | 1 << bit
        if high != low and high < count:
            route += [(low, high), (high, low)]
    return lax.ppermute(block, axis, route)


def join_halves(half, myself):
    other = partner(half, "heads", 0)
    low_first = jnp.concatenate([half, other], axis=1)
    high_first = jnp.concatenate([other, half], axis=1)
    return jnp.where(myself == 0, low_first, high_first)


def attention_rows(query, key_cache, value_cache, key_new, value_new, lengths):
    count = key_cache.shape[0]
    kv_local = key_cache.shape[1]
    slots = key_cache.shape[2]
    scale_factor = 1.0 / HD**0.5
    queries = query.reshape(count, kv_local, -1, HD)
    keys_all = jnp.concatenate([key_cache, key_new[:, :, None, :]], axis=2)
    values_all = jnp.concatenate([value_cache, value_new[:, :, None, :]], axis=2)
    scores = (
        jnp.einsum("rgjd,rgpd->rgjp", queries, keys_all, preferred_element_type=jnp.float32)
        * scale_factor
    )
    positions = jnp.arange(slots + 1, dtype=jnp.int32)[None, :]
    visible = ((positions < lengths[:, None]) | (positions == slots))[:, None, None, :]
    scores = jnp.where(visible, scores, -1e30)
    highest = jnp.max(scores, axis=-1)
    expons = jnp.where(visible, jnp.exp(scores - highest[..., None]), 0.0)
    totals = jnp.sum(expons, axis=-1)
    weights = (expons / totals[..., None]).astype(jnp.bfloat16)
    blended = jnp.einsum(
        "rgjp,rgpd->rgjd", weights, values_all, preferred_element_type=jnp.float32
    )
    return blended.reshape(count, -1)


def swiglu_rows(normed, gate_rows, up_rows, down_rows):
    gate = jnp.einsum("rd,nd->rn", normed, gate_rows, preferred_element_type=jnp.float32)
    upper = jnp.einsum("rd,nd->rn", normed, up_rows, preferred_element_type=jnp.float32)
    hidden = (jax.nn.silu(gate) * upper).astype(jnp.bfloat16)
    return jnp.dot(hidden, down_rows, preferred_element_type=jnp.float32)


def swiglu_halves(normed, gate_rows, up_rows, down_rows, myself, rows_shape):
    gate = jnp.einsum("rd,nd->rn", normed, gate_rows, preferred_element_type=jnp.float32)
    upper = jnp.einsum("rd,nd->rn", normed, up_rows, preferred_element_type=jnp.float32)
    hidden = (jax.nn.silu(gate) * upper).astype(jnp.bfloat16)
    hidden = hidden.reshape(rows_shape + hidden.shape[-1:])
    half_width = down_rows.shape[1] // 2
    down_given = lax.dynamic_slice_in_dim(down_rows, (1 - myself) * half_width, half_width, 1)
    down_kept = lax.dynamic_slice_in_dim(down_rows, myself * half_width, half_width, 1)
    given = jnp.einsum("...n,nd->...d", hidden, down_given, preferred_element_type=jnp.float32)
    kept = jnp.einsum("...n,nd->...d", hidden, down_kept, preferred_element_type=jnp.float32)
    return kept, given


def collect_rows(selector, returned):
    return lax.dot_general(
        selector,
        returned,
        (((0,), (0,)), ((), ())),
        precision=lax.Precision.HIGHEST,
        preferred_element_type=jnp.float32,
    )


def local(
    residual_in,
    query,
    key_cache,
    value_cache,
    key_new,
    value_new,
    lengths,
    norm_gain,
    hot_gate,
    hot_up,
    hot_down,
    cold_gate,
    cold_up,
    cold_down,
    active,
):
    attended = attention_rows(query, key_cache, value_cache, key_new, value_new, lengths)
    stream = (residual_in.astype(jnp.float32) + attended).astype(jnp.bfloat16)
    half_width = stream.shape[1]
    myself = lax.axis_index("heads")
    local_wide = stream.astype(jnp.float32)
    square_part = jnp.sum(local_wide * local_wide, axis=-1)
    square_total = square_part + partner(square_part, "heads", 0)
    gain_half = lax.dynamic_slice_in_dim(norm_gain, myself * half_width, half_width)
    scaled = (
        local_wide * lax.rsqrt(square_total / D + 1e-05)[:, None] * gain_half.astype(jnp.float32)
    )
    normed = join_halves(scaled.astype(jnp.bfloat16), myself)
    owner_count = lax.axis_size("rows")
    block_count = active.shape[1]
    request_count = active.shape[0]
    by_block = jnp.transpose(active)
    earlier = jnp.cumsum(by_block, axis=1) - by_block
    slot_ids = jnp.arange(CAP, dtype=jnp.int32)[None, :, None]
    slot_table = by_block[:, None, :] * (earlier[:, None, :] == slot_ids).astype(jnp.int32)
    selector3 = jnp.repeat(slot_table, owner_count // block_count, axis=0)
    selector = selector3.reshape(owner_count * CAP, request_count)
    outgoing = jnp.einsum(
        "ocr,rd->ocd",
        selector3.astype(jnp.bfloat16),
        scaled.astype(jnp.bfloat16),
        preferred_element_type=jnp.float32,
    ).astype(jnp.bfloat16)
    incoming_half = lax.all_to_all(outgoing, "rows", split_axis=0, concat_axis=0, tiled=True)
    incoming = join_halves(incoming_half.reshape(owner_count * CAP, -1), myself)
    kept, given = swiglu_halves(
        incoming, cold_gate, cold_up, cold_down, myself, (owner_count, CAP)
    )
    given_bf16 = given.astype(jnp.bfloat16)
    normed_late, given_bf16 = lax.optimization_barrier((normed, given_bf16))
    given_narrow = partner(given_bf16, "heads", 0)
    owner_sum = (kept + given_narrow.astype(jnp.float32)).astype(jnp.bfloat16)
    returned = lax.all_to_all(owner_sum, "rows", split_axis=0, concat_axis=0, tiled=True)
    hot_kept, hot_given = swiglu_halves(
        normed_late, hot_gate, hot_up, hot_down, myself, (request_count,)
    )
    hot_total = hot_kept + partner(hot_given, "heads", 0)
    cold_sum = collect_rows(
        selector.astype(jnp.float32),
        returned.reshape(owner_count * CAP, -1).astype(jnp.float32),
    )
    result = stream.astype(jnp.float32) + hot_total + cold_sum
    return result.astype(jnp.bfloat16)


def solution(mesh):
    return jax.shard_map(
        local,
        mesh=mesh,
        in_specs=(
            P(("groups", "rows"), "heads"),
            P(("groups", "rows"), "heads"),
            P(("groups", "rows"), "heads", None, None),
            P(("groups", "rows"), "heads", None, None),
            P(("groups", "rows"), "heads", None),
            P(("groups", "rows"), "heads", None),
            P(("groups", "rows")),
            P(),
            P("heads", None),
            P("heads", None),
            P("heads", None),
            P(("rows", "heads"), None),
            P(("rows", "heads"), None),
            P(("rows", "heads"), None),
            P(("groups", "rows"), None),
        ),
        out_specs=P(("groups", "rows"), "heads"),
        check_vma=False,
    )
```

```python
import jax
import jax.numpy as jnp
from jax import lax
from jax.sharding import PartitionSpec as P

HD = 128
D = 8192
CAP = 2


def partner(block, axis, bit):
    count = lax.axis_size(axis)
    route = []
    for low in range(count):
        high = low | 1 << bit
        if high != low and high < count:
            route += [(low, high), (high, low)]
    return lax.ppermute(block, axis, route)


def join_halves(half, myself):
    other = partner(half, "heads", 0)
    low_first = jnp.concatenate([half, other], axis=1)
    high_first = jnp.concatenate([other, half], axis=1)
    return jnp.where(myself == 0, low_first, high_first)


def attention_rows(query, key_cache, value_cache, key_new, value_new, lengths):
    count = key_cache.shape[0]
    kv_local = key_cache.shape[1]
    slots = key_cache.shape[2]
    scale_factor = 1.0 / HD**0.5
    queries = query.reshape(count, kv_local, -1, HD)
    keys_all = jnp.concatenate([key_cache, key_new[:, :, None, :]], axis=2)
    values_all = jnp.concatenate([value_cache, value_new[:, :, None, :]], axis=2)
    scores = (
        jnp.einsum("rgjd,rgpd->rgjp", queries, keys_all, preferred_element_type=jnp.float32)
        * scale_factor
    )
    positions = jnp.arange(slots + 1, dtype=jnp.int32)[None, :]
    visible = ((positions < lengths[:, None]) | (positions == slots))[:, None, None, :]
    scores = jnp.where(visible, scores, -1e30)
    highest = jnp.max(scores, axis=-1)
    expons = jnp.where(visible, jnp.exp(scores - highest[..., None]), 0.0)
    totals = jnp.sum(expons, axis=-1)
    weights = (expons / totals[..., None]).astype(jnp.bfloat16)
    blended = jnp.einsum(
        "rgjp,rgpd->rgjd", weights, values_all, preferred_element_type=jnp.float32
    )
    return blended.reshape(count, -1)


def swiglu_rows(normed, gate_rows, up_rows, down_rows):
    gate = jnp.einsum("rd,nd->rn", normed, gate_rows, preferred_element_type=jnp.float32)
    upper = jnp.einsum("rd,nd->rn", normed, up_rows, preferred_element_type=jnp.float32)
    hidden = (jax.nn.silu(gate) * upper).astype(jnp.bfloat16)
    return jnp.dot(hidden, down_rows, preferred_element_type=jnp.float32)


def swiglu_halves(normed, gate_rows, up_rows, down_rows, myself, rows_shape):
    gate = jnp.einsum("rd,nd->rn", normed, gate_rows, preferred_element_type=jnp.float32)
    upper = jnp.einsum("rd,nd->rn", normed, up_rows, preferred_element_type=jnp.float32)
    hidden = (jax.nn.silu(gate) * upper).astype(jnp.bfloat16)
    hidden = hidden.reshape(rows_shape + hidden.shape[-1:])
    half_width = down_rows.shape[1] // 2
    down_given = lax.dynamic_slice_in_dim(down_rows, (1 - myself) * half_width, half_width, 1)
    down_kept = lax.dynamic_slice_in_dim(down_rows, myself * half_width, half_width, 1)
    given = jnp.einsum("...n,nd->...d", hidden, down_given, preferred_element_type=jnp.float32)
    kept = jnp.einsum("...n,nd->...d", hidden, down_kept, preferred_element_type=jnp.float32)
    return kept, given


def split_dot(features_mine, features_other, rows, myself):
    width = features_mine.shape[1]
    rows_mine = lax.dynamic_slice_in_dim(rows, myself * width, width, 1)
    rows_other = lax.dynamic_slice_in_dim(rows, (1 - myself) * width, width, 1)
    first = jnp.einsum("rd,nd->rn", features_mine, rows_mine, preferred_element_type=jnp.float32)
    second = jnp.einsum("rd,nd->rn", features_other, rows_other, preferred_element_type=jnp.float32)
    return first + second


def swiglu_split(features_mine, features_other, gate_rows, up_rows, down_rows, myself, rows_shape):
    gate = split_dot(features_mine, features_other, gate_rows, myself)
    upper = split_dot(features_mine, features_other, up_rows, myself)
    hidden = (jax.nn.silu(gate) * upper).astype(jnp.bfloat16)
    hidden = hidden.reshape(rows_shape + hidden.shape[-1:])
    half_width = down_rows.shape[1] // 2
    down_given = lax.dynamic_slice_in_dim(down_rows, (1 - myself) * half_width, half_width, 1)
    down_kept = lax.dynamic_slice_in_dim(down_rows, myself * half_width, half_width, 1)
    given = jnp.einsum("...n,nd->...d", hidden, down_given, preferred_element_type=jnp.float32)
    kept = jnp.einsum("...n,nd->...d", hidden, down_kept, preferred_element_type=jnp.float32)
    return kept, given


def collect_rows(selector, returned):
    return lax.dot_general(
        selector,
        returned,
        (((0,), (0,)), ((), ())),
        precision=lax.Precision.HIGHEST,
        preferred_element_type=jnp.float32,
    )


def local(
    residual_in,
    query,
    key_cache,
    value_cache,
    key_new,
    value_new,
    lengths,
    norm_gain,
    hot_gate,
    hot_up,
    hot_down,
    cold_gate,
    cold_up,
    cold_down,
    active,
):
    attended = attention_rows(query, key_cache, value_cache, key_new, value_new, lengths)
    stream = (residual_in.astype(jnp.float32) + attended).astype(jnp.bfloat16)
    half_width = stream.shape[1]
    myself = lax.axis_index("heads")
    local_wide = stream.astype(jnp.float32)
    square_part = jnp.sum(local_wide * local_wide, axis=-1)
    square_total = square_part + partner(square_part, "heads", 0)
    gain_half = lax.dynamic_slice_in_dim(norm_gain, myself * half_width, half_width)
    scaled = (
        local_wide * lax.rsqrt(square_total / D + 1e-05)[:, None] * gain_half.astype(jnp.float32)
    )
    normed = join_halves(scaled.astype(jnp.bfloat16), myself)
    owner_count = lax.axis_size("rows")
    block_count = active.shape[1]
    request_count = active.shape[0]
    by_block = jnp.transpose(active)
    earlier = jnp.cumsum(by_block, axis=1) - by_block
    slot_ids = jnp.arange(CAP, dtype=jnp.int32)[None, :, None]
    slot_table = by_block[:, None, :] * (earlier[:, None, :] == slot_ids).astype(jnp.int32)
    selector3 = jnp.repeat(slot_table, owner_count // block_count, axis=0)
    selector = selector3.reshape(owner_count * CAP, request_count)
    outgoing = jnp.einsum(
        "ocr,rd->ocd",
        selector3.astype(jnp.bfloat16),
        scaled.astype(jnp.bfloat16),
        preferred_element_type=jnp.float32,
    ).astype(jnp.bfloat16)
    incoming_half = lax.all_to_all(outgoing, "rows", split_axis=0, concat_axis=0, tiled=True)
    features_mine = incoming_half.reshape(owner_count * CAP, -1)
    features_other = partner(features_mine, "heads", 0)
    kept, given = swiglu_split(
        features_mine, features_other, cold_gate, cold_up, cold_down, myself, (owner_count, CAP)
    )
    given_narrow = partner(given.astype(jnp.bfloat16), "heads", 0)
    owner_sum = (kept + given_narrow.astype(jnp.float32)).astype(jnp.bfloat16)
    normed_late, owner_sum = lax.optimization_barrier((normed, owner_sum))
    returned = lax.all_to_all(owner_sum, "rows", split_axis=0, concat_axis=0, tiled=True)
    hot_kept, hot_given = swiglu_halves(
        normed_late, hot_gate, hot_up, hot_down, myself, (request_count,)
    )
    hot_total = hot_kept + partner(hot_given, "heads", 0)
    cold_sum = collect_rows(
        selector.astype(jnp.float32),
        returned.reshape(owner_count * CAP, -1).astype(jnp.float32),
    )
    result = stream.astype(jnp.float32) + hot_total + cold_sum
    return result.astype(jnp.bfloat16)


def solution(mesh):
    return jax.shard_map(
        local,
        mesh=mesh,
        in_specs=(
            P(("groups", "rows"), "heads"),
            P(("groups", "rows"), "heads"),
            P(("groups", "rows"), "heads", None, None),
            P(("groups", "rows"), "heads", None, None),
            P(("groups", "rows"), "heads", None),
            P(("groups", "rows"), "heads", None),
            P(("groups", "rows")),
            P(),
            P("heads", None),
            P("heads", None),
            P("heads", None),
            P(("rows", "heads"), None),
            P(("rows", "heads"), None),
            P(("rows", "heads"), None),
            P(("groups", "rows"), None),
        ),
        out_specs=P(("groups", "rows"), "heads"),
        check_vma=False,
    )
```

```python
import jax
import jax.numpy as jnp
from jax import lax
from jax.sharding import PartitionSpec as P

HD = 128
D = 8192
CAP = 2


def partner(block, axis, bit):
    count = lax.axis_size(axis)
    route = []
    for low in range(count):
        high = low | 1 << bit
        if high != low and high < count:
            route += [(low, high), (high, low)]
    return lax.ppermute(block, axis, route)


def join_halves(half, myself):
    other = partner(half, "heads", 0)
    low_first = jnp.concatenate([half, other], axis=1)
    high_first = jnp.concatenate([other, half], axis=1)
    return jnp.where(myself == 0, low_first, high_first)


def attention_rows(query, key_cache, value_cache, key_new, value_new, lengths):
    count = key_cache.shape[0]
    kv_local = key_cache.shape[1]
    slots = key_cache.shape[2]
    scale_factor = 1.0 / HD**0.5
    queries = query.reshape(count, kv_local, -1, HD)
    copies = (count, kv_local, 8, HD)
    keys_all = jnp.concatenate(
        [key_cache, jnp.broadcast_to(key_new[:, :, None, :], copies)], axis=2
    )
    values_all = jnp.concatenate(
        [value_cache, jnp.broadcast_to(value_new[:, :, None, :], copies)], axis=2
    )
    scores = lax.optimization_barrier(
        jnp.einsum("rgjd,rgpd->rgjp", queries, keys_all, preferred_element_type=jnp.float32)
        * scale_factor
    )
    positions = jnp.arange(slots + 8, dtype=jnp.int32)[None, :]
    visible = ((positions < lengths[:, None]) | (positions == slots))[:, None, None, :]
    scores = jnp.where(visible, scores, -1e30)
    highest = jnp.max(scores, axis=-1)
    expons = jnp.where(visible, jnp.exp(scores - highest[..., None]), 0.0)
    totals = jnp.sum(expons, axis=-1)
    weights = (expons / totals[..., None]).astype(jnp.bfloat16)
    blended = jnp.einsum(
        "rgjp,rgpd->rgjd", weights, values_all, preferred_element_type=jnp.float32
    )
    return blended.reshape(count, -1)


def swiglu_rows(normed, gate_rows, up_rows, down_rows):
    gate = jnp.einsum("rd,nd->rn", normed, gate_rows, preferred_element_type=jnp.float32)
    upper = jnp.einsum("rd,nd->rn", normed, up_rows, preferred_element_type=jnp.float32)
    hidden = (jax.nn.silu(gate) * upper).astype(jnp.bfloat16)
    return jnp.dot(hidden, down_rows, preferred_element_type=jnp.float32)


def swiglu_halves(normed, gate_rows, up_rows, down_rows, myself, rows_shape):
    gate = jnp.einsum("rd,nd->rn", normed, gate_rows, preferred_element_type=jnp.float32)
    upper = jnp.einsum("rd,nd->rn", normed, up_rows, preferred_element_type=jnp.float32)
    hidden = (jax.nn.silu(gate) * upper).astype(jnp.bfloat16)
    hidden = hidden.reshape(rows_shape + hidden.shape[-1:])
    half_width = down_rows.shape[1] // 2
    down_given = lax.dynamic_slice_in_dim(down_rows, (1 - myself) * half_width, half_width, 1)
    down_kept = lax.dynamic_slice_in_dim(down_rows, myself * half_width, half_width, 1)
    given = jnp.einsum("...n,nd->...d", hidden, down_given, preferred_element_type=jnp.float32)
    kept = jnp.einsum("...n,nd->...d", hidden, down_kept, preferred_element_type=jnp.float32)
    return kept, given


def collect_rows(selector, returned):
    return lax.dot_general(
        selector,
        returned,
        (((0,), (0,)), ((), ())),
        precision=lax.Precision.HIGHEST,
        preferred_element_type=jnp.float32,
    )


def local(
    residual_in,
    query,
    key_cache,
    value_cache,
    key_new,
    value_new,
    lengths,
    norm_gain,
    hot_gate,
    hot_up,
    hot_down,
    cold_gate,
    cold_up,
    cold_down,
    active,
):
    attended = attention_rows(query, key_cache, value_cache, key_new, value_new, lengths)
    stream = (residual_in.astype(jnp.float32) + attended).astype(jnp.bfloat16)
    half_width = stream.shape[1]
    myself = lax.axis_index("heads")
    local_wide = stream.astype(jnp.float32)
    square_part = jnp.sum(local_wide * local_wide, axis=-1)
    square_total = square_part + partner(square_part, "heads", 0)
    gain_half = lax.dynamic_slice_in_dim(norm_gain, myself * half_width, half_width)
    scaled = (
        local_wide * lax.rsqrt(square_total / D + 1e-05)[:, None] * gain_half.astype(jnp.float32)
    )
    normed = join_halves(scaled.astype(jnp.bfloat16), myself)
    owner_count = lax.axis_size("rows")
    block_count = active.shape[1]
    request_count = active.shape[0]
    by_block = jnp.transpose(active)
    earlier = jnp.cumsum(by_block, axis=1) - by_block
    slot_ids = jnp.arange(CAP, dtype=jnp.int32)[None, :, None]
    slot_table = by_block[:, None, :] * (earlier[:, None, :] == slot_ids).astype(jnp.int32)
    selector3 = jnp.repeat(slot_table, owner_count // block_count, axis=0)
    selector = selector3.reshape(owner_count * CAP, request_count)
    outgoing = jnp.einsum(
        "ocr,rd->ocd",
        selector3.astype(jnp.bfloat16),
        scaled.astype(jnp.bfloat16),
        preferred_element_type=jnp.float32,
    ).astype(jnp.bfloat16)
    incoming_half = lax.all_to_all(outgoing, "rows", split_axis=0, concat_axis=0, tiled=True)
    incoming = join_halves(incoming_half.reshape(owner_count * CAP, -1), myself)
    kept, given = swiglu_halves(
        incoming, cold_gate, cold_up, cold_down, myself, (owner_count, CAP)
    )
    given_narrow = partner(given.astype(jnp.bfloat16), "heads", 0)
    owner_sum = (kept + given_narrow.astype(jnp.float32)).astype(jnp.bfloat16)
    normed_late, owner_sum = lax.optimization_barrier((normed, owner_sum))
    returned = lax.all_to_all(owner_sum, "rows", split_axis=0, concat_axis=0, tiled=True)
    hot_kept, hot_given = swiglu_halves(
        normed_late, hot_gate, hot_up, hot_down, myself, (request_count,)
    )
    hot_received = partner(hot_given, "heads", 0)
    settled = lax.optimization_barrier(stream.astype(jnp.float32) + hot_kept)
    cold_sum = collect_rows(
        selector.astype(jnp.float32),
        returned.reshape(owner_count * CAP, -1).astype(jnp.float32),
    )
    result = settled + hot_received + cold_sum
    return result.astype(jnp.bfloat16)


def solution(mesh):
    return jax.shard_map(
        local,
        mesh=mesh,
        in_specs=(
            P(("groups", "rows"), "heads"),
            P(("groups", "rows"), "heads"),
            P(("groups", "rows"), "heads", None, None),
            P(("groups", "rows"), "heads", None, None),
            P(("groups", "rows"), "heads", None),
            P(("groups", "rows"), "heads", None),
            P(("groups", "rows")),
            P(),
            P("heads", None),
            P("heads", None),
            P("heads", None),
            P(("rows", "heads"), None),
            P(("rows", "heads"), None),
            P(("rows", "heads"), None),
            P(("groups", "rows"), None),
        ),
        out_specs=P(("groups", "rows"), "heads"),
        check_vma=False,
    )
```

```python
import jax
import jax.numpy as jnp
from jax import lax
from jax.sharding import PartitionSpec as P

HD = 128
D = 8192
CAP = 2


def partner(block, axis, bit):
    count = lax.axis_size(axis)
    route = []
    for low in range(count):
        high = low | 1 << bit
        if high != low and high < count:
            route += [(low, high), (high, low)]
    return lax.ppermute(block, axis, route)


def join_halves(half, myself):
    other = partner(half, "heads", 0)
    low_first = jnp.concatenate([half, other], axis=1)
    high_first = jnp.concatenate([other, half], axis=1)
    return jnp.where(myself == 0, low_first, high_first)


def attention_rows(query, key_cache, value_cache, key_new, value_new, lengths):
    count = key_cache.shape[0]
    kv_local = key_cache.shape[1]
    slots = key_cache.shape[2]
    scale_factor = 1.0 / HD**0.5
    queries = query.reshape(count, kv_local, -1, HD)
    copies = (count, kv_local, 8, HD)
    keys_all = jnp.concatenate(
        [key_cache, jnp.broadcast_to(key_new[:, :, None, :], copies)], axis=2
    )
    values_all = jnp.concatenate(
        [value_cache, jnp.broadcast_to(value_new[:, :, None, :], copies)], axis=2
    )
    scores, values_all = lax.optimization_barrier(
        (
            jnp.einsum("rgjd,rgpd->rgjp", queries, keys_all, preferred_element_type=jnp.float32)
            * scale_factor,
            values_all,
        )
    )
    positions = jnp.arange(slots + 8, dtype=jnp.int32)[None, :]
    visible = ((positions < lengths[:, None]) | (positions == slots))[:, None, None, :]
    scores = jnp.where(visible, scores, -1e30)
    highest = jnp.max(scores, axis=-1)
    expons = jnp.where(visible, jnp.exp(scores - highest[..., None]), 0.0)
    totals = jnp.sum(expons, axis=-1)
    weights = (expons / totals[..., None]).astype(jnp.bfloat16)
    blended = jnp.einsum(
        "rgjp,rgpd->rgjd", weights, values_all, preferred_element_type=jnp.float32
    )
    return blended.reshape(count, -1)


def swiglu_rows(normed, gate_rows, up_rows, down_rows):
    gate = jnp.einsum("rd,nd->rn", normed, gate_rows, preferred_element_type=jnp.float32)
    upper = jnp.einsum("rd,nd->rn", normed, up_rows, preferred_element_type=jnp.float32)
    hidden = (jax.nn.silu(gate) * upper).astype(jnp.bfloat16)
    return jnp.dot(hidden, down_rows, preferred_element_type=jnp.float32)


def swiglu_halves(normed, gate_rows, up_rows, down_rows, myself, rows_shape):
    gate = jnp.einsum("rd,nd->rn", normed, gate_rows, preferred_element_type=jnp.float32)
    upper = jnp.einsum("rd,nd->rn", normed, up_rows, preferred_element_type=jnp.float32)
    hidden = (jax.nn.silu(gate) * upper).astype(jnp.bfloat16)
    hidden = hidden.reshape(rows_shape + hidden.shape[-1:])
    half_width = down_rows.shape[1] // 2
    down_given = lax.dynamic_slice_in_dim(down_rows, (1 - myself) * half_width, half_width, 1)
    down_kept = lax.dynamic_slice_in_dim(down_rows, myself * half_width, half_width, 1)
    given = jnp.einsum("...n,nd->...d", hidden, down_given, preferred_element_type=jnp.float32)
    kept = jnp.einsum("...n,nd->...d", hidden, down_kept, preferred_element_type=jnp.float32)
    return kept, given


def collect_rows(selector, returned):
    return lax.dot_general(
        selector,
        returned,
        (((0,), (0,)), ((), ())),
        precision=lax.Precision.HIGHEST,
        preferred_element_type=jnp.float32,
    )


def local(
    residual_in,
    query,
    key_cache,
    value_cache,
    key_new,
    value_new,
    lengths,
    norm_gain,
    hot_gate,
    hot_up,
    hot_down,
    cold_gate,
    cold_up,
    cold_down,
    active,
):
    attended = attention_rows(query, key_cache, value_cache, key_new, value_new, lengths)
    stream = (residual_in.astype(jnp.float32) + attended).astype(jnp.bfloat16)
    half_width = stream.shape[1]
    myself = lax.axis_index("heads")
    local_wide = stream.astype(jnp.float32)
    square_part = jnp.sum(local_wide * local_wide, axis=-1)
    square_total = square_part + partner(square_part, "heads", 0)
    gain_half = lax.dynamic_slice_in_dim(norm_gain, myself * half_width, half_width)
    scaled = (
        local_wide * lax.rsqrt(square_total / D + 1e-05)[:, None] * gain_half.astype(jnp.float32)
    )
    normed = join_halves(scaled.astype(jnp.bfloat16), myself)
    owner_count = lax.axis_size("rows")
    block_count = active.shape[1]
    request_count = active.shape[0]
    by_block = jnp.transpose(active)
    earlier = jnp.cumsum(by_block, axis=1) - by_block
    slot_ids = jnp.arange(CAP, dtype=jnp.int32)[None, :, None]
    slot_table = by_block[:, None, :] * (earlier[:, None, :] == slot_ids).astype(jnp.int32)
    selector3 = jnp.repeat(slot_table, owner_count // block_count, axis=0)
    selector = selector3.reshape(owner_count * CAP, request_count)
    outgoing = jnp.einsum(
        "ocr,rd->ocd",
        selector3.astype(jnp.bfloat16),
        scaled.astype(jnp.bfloat16),
        preferred_element_type=jnp.float32,
    ).astype(jnp.bfloat16)
    incoming_half = lax.all_to_all(outgoing, "rows", split_axis=0, concat_axis=0, tiled=True)
    incoming = join_halves(incoming_half.reshape(owner_count * CAP, -1), myself)
    kept, given = swiglu_halves(
        incoming, cold_gate, cold_up, cold_down, myself, (owner_count, CAP)
    )
    given_narrow = partner(given.astype(jnp.bfloat16), "heads", 0)
    owner_sum = (kept + given_narrow.astype(jnp.float32)).astype(jnp.bfloat16)
    normed_late, owner_sum = lax.optimization_barrier((normed, owner_sum))
    returned = lax.all_to_all(owner_sum, "rows", split_axis=0, concat_axis=0, tiled=True)
    hot_kept, hot_given = swiglu_halves(
        normed_late, hot_gate, hot_up, hot_down, myself, (request_count,)
    )
    hot_received = partner(hot_given, "heads", 0)
    settled = lax.optimization_barrier(stream.astype(jnp.float32) + hot_kept)
    cold_sum = collect_rows(
        selector.astype(jnp.float32),
        returned.reshape(owner_count * CAP, -1).astype(jnp.float32),
    )
    result = settled + hot_received + cold_sum
    return result.astype(jnp.bfloat16)


def solution(mesh):
    return jax.shard_map(
        local,
        mesh=mesh,
        in_specs=(
            P(("groups", "rows"), "heads"),
            P(("groups", "rows"), "heads"),
            P(("groups", "rows"), "heads", None, None),
            P(("groups", "rows"), "heads", None, None),
            P(("groups", "rows"), "heads", None),
            P(("groups", "rows"), "heads", None),
            P(("groups", "rows")),
            P(),
            P("heads", None),
            P("heads", None),
            P("heads", None),
            P(("rows", "heads"), None),
            P(("rows", "heads"), None),
            P(("rows", "heads"), None),
            P(("groups", "rows"), None),
        ),
        out_specs=P(("groups", "rows"), "heads"),
        check_vma=False,
    )
```

```python
import jax
import jax.numpy as jnp
from jax import lax
from jax.sharding import PartitionSpec as P

HD = 128
D = 8192
CAP = 2


def partner(block, axis, bit):
    count = lax.axis_size(axis)
    route = []
    for low in range(count):
        high = low | 1 << bit
        if high != low and high < count:
            route += [(low, high), (high, low)]
    return lax.ppermute(block, axis, route)


def join_halves(half, myself):
    other = partner(half, "heads", 0)
    low_first = jnp.concatenate([half, other], axis=1)
    high_first = jnp.concatenate([other, half], axis=1)
    return jnp.where(myself == 0, low_first, high_first)


def attention_rows(query, key_cache, value_cache, key_new, value_new, lengths, residual):
    count = key_cache.shape[0]
    kv_local = key_cache.shape[1]
    slots = key_cache.shape[2]
    scale_factor = 1.0 / HD**0.5
    queries = query.reshape(count, kv_local, -1, HD)
    copies = (count, kv_local, 8, HD)
    keys_all = jnp.concatenate(
        [key_cache, jnp.broadcast_to(key_new[:, :, None, :], copies)], axis=2
    )
    values_all = jnp.concatenate(
        [value_cache, jnp.broadcast_to(value_new[:, :, None, :], copies)], axis=2
    )
    scores, values_all, residual_wide = lax.optimization_barrier(
        (
            jnp.einsum("rgjd,rgpd->rgjp", queries, keys_all, preferred_element_type=jnp.float32)
            * scale_factor,
            values_all,
            residual.astype(jnp.float32),
        )
    )
    positions = jnp.arange(slots + 8, dtype=jnp.int32)[None, :]
    visible = ((positions < lengths[:, None]) | (positions == slots))[:, None, None, :]
    scores = jnp.where(visible, scores, -1e30)
    highest = jnp.max(scores, axis=-1)
    expons = jnp.where(visible, jnp.exp(scores - highest[..., None]), 0.0)
    totals = jnp.sum(expons, axis=-1)
    weights = (expons / totals[..., None]).astype(jnp.bfloat16)
    blended = jnp.einsum(
        "rgjp,rgpd->rgjd", weights, values_all, preferred_element_type=jnp.float32
    )
    return residual_wide + blended.reshape(count, -1)


def swiglu_rows(normed, gate_rows, up_rows, down_rows):
    gate = jnp.einsum("rd,nd->rn", normed, gate_rows, preferred_element_type=jnp.float32)
    upper = jnp.einsum("rd,nd->rn", normed, up_rows, preferred_element_type=jnp.float32)
    hidden = (jax.nn.silu(gate) * upper).astype(jnp.bfloat16)
    return jnp.dot(hidden, down_rows, preferred_element_type=jnp.float32)


def swiglu_halves(normed, gate_rows, up_rows, down_rows, myself, rows_shape):
    gate = jnp.einsum("rd,nd->rn", normed, gate_rows, preferred_element_type=jnp.float32)
    upper = jnp.einsum("rd,nd->rn", normed, up_rows, preferred_element_type=jnp.float32)
    hidden = (jax.nn.silu(gate) * upper).astype(jnp.bfloat16)
    hidden = hidden.reshape(rows_shape + hidden.shape[-1:])
    half_width = down_rows.shape[1] // 2
    down_given = lax.dynamic_slice_in_dim(down_rows, (1 - myself) * half_width, half_width, 1)
    down_kept = lax.dynamic_slice_in_dim(down_rows, myself * half_width, half_width, 1)
    given = jnp.einsum("...n,nd->...d", hidden, down_given, preferred_element_type=jnp.float32)
    kept = jnp.einsum("...n,nd->...d", hidden, down_kept, preferred_element_type=jnp.float32)
    return kept, given


def collect_rows(selector, returned):
    return lax.dot_general(
        selector,
        returned,
        (((0,), (0,)), ((), ())),
        precision=lax.Precision.HIGHEST,
        preferred_element_type=jnp.float32,
    )


def local(
    residual_in,
    query,
    key_cache,
    value_cache,
    key_new,
    value_new,
    lengths,
    norm_gain,
    hot_gate,
    hot_up,
    hot_down,
    cold_gate,
    cold_up,
    cold_down,
    active,
):
    stream = attention_rows(
        query, key_cache, value_cache, key_new, value_new, lengths, residual_in
    ).astype(jnp.bfloat16)
    half_width = stream.shape[1]
    myself = lax.axis_index("heads")
    local_wide = stream.astype(jnp.float32)
    square_part = jnp.sum(local_wide * local_wide, axis=-1)
    square_total = square_part + partner(square_part, "heads", 0)
    gain_half = lax.dynamic_slice_in_dim(norm_gain, myself * half_width, half_width)
    scaled = (
        local_wide * lax.rsqrt(square_total / D + 1e-05)[:, None] * gain_half.astype(jnp.float32)
    )
    normed = join_halves(scaled.astype(jnp.bfloat16), myself)
    owner_count = lax.axis_size("rows")
    block_count = active.shape[1]
    request_count = active.shape[0]
    by_block = jnp.transpose(active)
    earlier = jnp.cumsum(by_block, axis=1) - by_block
    slot_ids = jnp.arange(CAP, dtype=jnp.int32)[None, :, None]
    slot_table = by_block[:, None, :] * (earlier[:, None, :] == slot_ids).astype(jnp.int32)
    selector3 = jnp.repeat(slot_table, owner_count // block_count, axis=0)
    selector = selector3.reshape(owner_count * CAP, request_count)
    outgoing = jnp.einsum(
        "ocr,rd->ocd",
        selector3.astype(jnp.bfloat16),
        scaled.astype(jnp.bfloat16),
        preferred_element_type=jnp.float32,
    ).astype(jnp.bfloat16)
    incoming_half = lax.all_to_all(outgoing, "rows", split_axis=0, concat_axis=0, tiled=True)
    incoming = join_halves(incoming_half.reshape(owner_count * CAP, -1), myself)
    kept, given = swiglu_halves(
        incoming, cold_gate, cold_up, cold_down, myself, (owner_count, CAP)
    )
    given_narrow = partner(given.astype(jnp.bfloat16), "heads", 0)
    owner_sum = (kept + given_narrow.astype(jnp.float32)).astype(jnp.bfloat16)
    normed_late, owner_sum = lax.optimization_barrier((normed, owner_sum))
    returned = lax.all_to_all(owner_sum, "rows", split_axis=0, concat_axis=0, tiled=True)
    hot_kept, hot_given = swiglu_halves(
        normed_late, hot_gate, hot_up, hot_down, myself, (request_count,)
    )
    hot_received = partner(hot_given, "heads", 0)
    settled = lax.optimization_barrier(stream.astype(jnp.float32) + hot_kept)
    cold_sum = collect_rows(
        selector.astype(jnp.float32),
        returned.reshape(owner_count * CAP, -1).astype(jnp.float32),
    )
    result = settled + hot_received + cold_sum
    return result.astype(jnp.bfloat16)


def solution(mesh):
    return jax.shard_map(
        local,
        mesh=mesh,
        in_specs=(
            P(("groups", "rows"), "heads"),
            P(("groups", "rows"), "heads"),
            P(("groups", "rows"), "heads", None, None),
            P(("groups", "rows"), "heads", None, None),
            P(("groups", "rows"), "heads", None),
            P(("groups", "rows"), "heads", None),
            P(("groups", "rows")),
            P(),
            P("heads", None),
            P("heads", None),
            P("heads", None),
            P(("rows", "heads"), None),
            P(("rows", "heads"), None),
            P(("rows", "heads"), None),
            P(("groups", "rows"), None),
        ),
        out_specs=P(("groups", "rows"), "heads"),
        check_vma=False,
    )
```

```python
import jax
import jax.numpy as jnp
from jax import lax
from jax.sharding import PartitionSpec as P

HD = 128
D = 8192
CAP = 2


def partner(block, axis, bit):
    count = lax.axis_size(axis)
    route = []
    for low in range(count):
        high = low | 1 << bit
        if high != low and high < count:
            route += [(low, high), (high, low)]
    return lax.ppermute(block, axis, route)


def join_halves(half, myself):
    other = partner(half, "heads", 0)
    low_first = jnp.concatenate([half, other], axis=1)
    high_first = jnp.concatenate([other, half], axis=1)
    return jnp.where(myself == 0, low_first, high_first)


def attention_rows(query, key_cache, value_cache, key_new, value_new, lengths, residual):
    count = key_cache.shape[0]
    kv_local = key_cache.shape[1]
    slots = key_cache.shape[2]
    scale_factor = 1.0 / HD**0.5
    queries = query.reshape(count, kv_local, -1, HD)
    copies = (count, kv_local, 8, HD)
    keys_all = jnp.concatenate(
        [key_cache, jnp.broadcast_to(key_new[:, :, None, :], copies)], axis=2
    )
    values_all = jnp.concatenate(
        [value_cache, jnp.broadcast_to(value_new[:, :, None, :], copies)], axis=2
    )
    positions = jnp.arange(slots + 8, dtype=jnp.int32)[None, :]
    visible = (positions < lengths[:, None]) | (positions == slots)
    scores, values_all, residual_wide, visible = lax.optimization_barrier(
        (
            jnp.einsum("rgjd,rgpd->rgjp", queries, keys_all, preferred_element_type=jnp.float32)
            * scale_factor,
            values_all,
            residual.astype(jnp.float32),
            visible,
        )
    )
    visible = visible[:, None, None, :]
    scores = jnp.where(visible, scores, -1e30)
    highest = jnp.max(scores, axis=-1)
    expons = jnp.where(visible, jnp.exp(scores - highest[..., None]), 0.0)
    totals = jnp.sum(expons, axis=-1)
    weights = (expons / totals[..., None]).astype(jnp.bfloat16)
    blended = jnp.einsum(
        "rgjp,rgpd->rgjd", weights, values_all, preferred_element_type=jnp.float32
    )
    return residual_wide + blended.reshape(count, -1)


def swiglu_rows(normed, gate_rows, up_rows, down_rows):
    gate = jnp.einsum("rd,nd->rn", normed, gate_rows, preferred_element_type=jnp.float32)
    upper = jnp.einsum("rd,nd->rn", normed, up_rows, preferred_element_type=jnp.float32)
    hidden = (jax.nn.silu(gate) * upper).astype(jnp.bfloat16)
    return jnp.dot(hidden, down_rows, preferred_element_type=jnp.float32)


def swiglu_halves(normed, gate_rows, up_rows, down_rows, myself, rows_shape):
    gate = jnp.einsum("rd,nd->rn", normed, gate_rows, preferred_element_type=jnp.float32)
    upper = jnp.einsum("rd,nd->rn", normed, up_rows, preferred_element_type=jnp.float32)
    hidden = (jax.nn.silu(gate) * upper).astype(jnp.bfloat16)
    hidden = hidden.reshape(rows_shape + hidden.shape[-1:])
    half_width = down_rows.shape[1] // 2
    down_given = lax.dynamic_slice_in_dim(down_rows, (1 - myself) * half_width, half_width, 1)
    down_kept = lax.dynamic_slice_in_dim(down_rows, myself * half_width, half_width, 1)
    given = jnp.einsum("...n,nd->...d", hidden, down_given, preferred_element_type=jnp.float32)
    kept = jnp.einsum("...n,nd->...d", hidden, down_kept, preferred_element_type=jnp.float32)
    return kept, given


def collect_rows(selector, returned):
    return lax.dot_general(
        selector,
        returned,
        (((0,), (0,)), ((), ())),
        precision=lax.Precision.HIGHEST,
        preferred_element_type=jnp.float32,
    )


def local(
    residual_in,
    query,
    key_cache,
    value_cache,
    key_new,
    value_new,
    lengths,
    norm_gain,
    hot_gate,
    hot_up,
    hot_down,
    cold_gate,
    cold_up,
    cold_down,
    active,
):
    stream = attention_rows(
        query, key_cache, value_cache, key_new, value_new, lengths, residual_in
    ).astype(jnp.bfloat16)
    half_width = stream.shape[1]
    myself = lax.axis_index("heads")
    local_wide = stream.astype(jnp.float32)
    square_part = jnp.sum(local_wide * local_wide, axis=-1)
    square_total = square_part + partner(square_part, "heads", 0)
    gain_half = lax.dynamic_slice_in_dim(norm_gain, myself * half_width, half_width)
    scaled = (
        local_wide * lax.rsqrt(square_total / D + 1e-05)[:, None] * gain_half.astype(jnp.float32)
    )
    normed = join_halves(scaled.astype(jnp.bfloat16), myself)
    owner_count = lax.axis_size("rows")
    block_count = active.shape[1]
    request_count = active.shape[0]
    by_block = jnp.transpose(active)
    earlier = jnp.cumsum(by_block, axis=1) - by_block
    slot_ids = jnp.arange(CAP, dtype=jnp.int32)[None, :, None]
    slot_table = by_block[:, None, :] * (earlier[:, None, :] == slot_ids).astype(jnp.int32)
    selector3 = jnp.repeat(slot_table, owner_count // block_count, axis=0)
    selector = selector3.reshape(owner_count * CAP, request_count)
    outgoing = jnp.einsum(
        "ocr,rd->ocd",
        selector3.astype(jnp.bfloat16),
        scaled.astype(jnp.bfloat16),
        preferred_element_type=jnp.float32,
    ).astype(jnp.bfloat16)
    incoming_half = lax.all_to_all(outgoing, "rows", split_axis=0, concat_axis=0, tiled=True)
    incoming = join_halves(incoming_half.reshape(owner_count * CAP, -1), myself)
    kept, given = swiglu_halves(
        incoming, cold_gate, cold_up, cold_down, myself, (owner_count, CAP)
    )
    given_narrow = partner(given.astype(jnp.bfloat16), "heads", 0)
    owner_sum = (kept + given_narrow.astype(jnp.float32)).astype(jnp.bfloat16)
    normed_late, owner_sum = lax.optimization_barrier((normed, owner_sum))
    returned = lax.all_to_all(owner_sum, "rows", split_axis=0, concat_axis=0, tiled=True)
    hot_kept, hot_given = swiglu_halves(
        normed_late, hot_gate, hot_up, hot_down, myself, (request_count,)
    )
    hot_received = partner(hot_given, "heads", 0)
    settled = lax.optimization_barrier(stream.astype(jnp.float32) + hot_kept)
    cold_sum = collect_rows(
        selector.astype(jnp.float32),
        returned.reshape(owner_count * CAP, -1).astype(jnp.float32),
    )
    result = settled + hot_received + cold_sum
    return result.astype(jnp.bfloat16)


def solution(mesh):
    return jax.shard_map(
        local,
        mesh=mesh,
        in_specs=(
            P(("groups", "rows"), "heads"),
            P(("groups", "rows"), "heads"),
            P(("groups", "rows"), "heads", None, None),
            P(("groups", "rows"), "heads", None, None),
            P(("groups", "rows"), "heads", None),
            P(("groups", "rows"), "heads", None),
            P(("groups", "rows")),
            P(),
            P("heads", None),
            P("heads", None),
            P("heads", None),
            P(("rows", "heads"), None),
            P(("rows", "heads"), None),
            P(("rows", "heads"), None),
            P(("groups", "rows"), None),
        ),
        out_specs=P(("groups", "rows"), "heads"),
        check_vma=False,
    )
```
